32 devices in a mesh: segment: 4 (over x, core), dp: 8 (over z, y).
Axes of the slice: x: 2, y: 2, z: 4, core: 2. Of those that a mesh axis runs over, the one named last changes fastest.
Arguments:
- inputs: bfloat16 [4, 8, 4, 16, 256], P(None, 'dp'), may hold values from -6 to 6
- out_grad: bfloat16 [4, 8, 4, 16, 256], P(None, 'dp'), may hold values from -6 to 6
- w_in: bfloat16 [4, 256, 1024], P('segment'), may hold values from -0.375 to 0.375
- w_out: bfloat16 [4, 1024, 256], P('segment'), may hold values from -0.1875 to 0.1875
- vector_params: float32 [4, 58, 256], P('segment'), may hold values from -2 to 2, as said below
Outputs:
- input_grads: bfloat16 [4, 4, 8, 4, 16, 256], P('segment', None, 'dp')
- step_w_in: float32 [4, 256, 1024], P('segment')
- step_w_out: float32 [4, 1024, 256], P('segment')
- step_vectors: float32 [4, 58, 256], P('segment')
The draws below stay inside these ranges and needn't reach their ends.
Inputs may be any that keep to these rules, and one draw needn't show every extreme that they name: `vector_params`: rows 0 to 48 are taps of order 0.2, row 50 lies in 0.5 to 1.5, row 53 in 0.2 to 1, the other rows are biases of order 0.5.
All inputs are finite; a program needn't handle non-finite values.
Results may differ from the reference program's by a relative error of at most 0.0095.
Values may be sent and summed in bfloat16 or wider, within the bound.
No kernel may reach another device: no remote copies, remote signals or barrier semaphores. Data moves between devices by JAX's collectives and lax.ppermute only.
A program may use at most 128 MiB of HBM per device.

```python
import jax
import jax.numpy as jnp
from jax import lax

C = 256
H = 4
W = 16
MB = 4
VROWS = 58
SAMPLES = 8
PARAMS = 2156544
N_SEGMENT = 4


def draw_vector_params(key, part):
    shape = (N_SEGMENT, VROWS, C)
    normal_part = jnp.clip(jax.random.normal(jax.random.fold_in(key, 11), shape, jnp.float32), -4.0, 4.0)
    even_part = jax.random.uniform(jax.random.fold_in(key, 12), shape, jnp.float32)
    base = normal_part
    kernel = 0.2 * base
    biases = 0.5 * base
    gains = 0.5 + even_part
    scales = jnp.exp(jnp.log(0.2) + even_part * jnp.log(5.0))
    rows = jnp.arange(VROWS)[None, :, None]
    chosen = jnp.where(rows < 49, kernel, jnp.where(rows == 50, gains, jnp.where(rows == 53, scales, biases)))
    return chosen.astype(jnp.float32)


def steps_of(rng, extent, shards, least, largest):
    loudness = 1.0
    for position, parts in shards:
        heights = jax.random.uniform(jax.random.fold_in(jax.random.fold_in(rng, 6), position), (parts,), jnp.float32, least / len(shards), largest / len(shards))
        loudness = loudness * jnp.repeat(jnp.exp(heights), extent[position] // parts).reshape((-1,) + (1,) * (len(extent) - 1 - position))
    return loudness


def scatter_about(stream_key, extent, scale, reach, cuts=(), kind=jnp.bfloat16):
    level = steps_of(stream_key, extent, cuts, -0.22, 0.18) if cuts else 1.0
    entries = jax.random.normal(stream_key, extent, jnp.float32) * scale * level
    return jnp.minimum(jnp.maximum(entries, -reach), reach).astype(kind)


def setup_inputs(seed: int = 0) -> dict:
    seeds = jax.random.split(jax.random.key(seed), 6)
    inputs = scatter_about(seeds[0], (MB, SAMPLES, H, W, C), 1.0, 6.0, ((1, 8),))
    out_grad = scatter_about(seeds[1], (MB, SAMPLES, H, W, C), 1.0, 6.0, ((1, 8),))
    w_in = scatter_about(seeds[2], (N_SEGMENT, C, 4 * C), C ** -0.5, 0.375, ((0, 4),))
    w_out = scatter_about(seeds[3], (N_SEGMENT, 4 * C, C), (4 * C) ** -0.5, 0.1875, ((0, 4),))
    vector_params = draw_vector_params(jax.random.fold_in(seeds[5], 71), 0)
    return {"inputs": inputs, "out_grad": out_grad, "w_in": w_in, "w_out": w_out, "vector_params": vector_params}


def depthwise(features, vectors):
    height = features.shape[1]
    breadth = features.shape[2]
    padded = jnp.pad(features, ((0, 0), (3, 3), (3, 3), (0, 0)))
    summed = jnp.zeros(features.shape, jnp.float32)
    for row_shift in range(7):
        for col_shift in range(7):
            summed = summed + padded[:, row_shift:row_shift + height, col_shift:col_shift + breadth, :] * vectors[row_shift * 7 + col_shift]
    return summed + vectors[49]

def normalize(features, vectors):
    conv = depthwise(features, vectors)
    average = lax.optimization_barrier(jnp.mean(conv, axis=-1, keepdims=True))
    centered = conv - average
    variance = lax.optimization_barrier(jnp.mean(centered * centered, axis=-1, keepdims=True))
    return centered * lax.rsqrt(variance + 1e-06) * vectors[50] + vectors[51]

def gelu_slope(preact):
    cumulative = 0.5 * (1.0 + jax.scipy.special.erf(preact * 0.7071067811865476))
    return cumulative + preact * jnp.exp(-0.5 * preact * preact) * 0.3989422804014327

def forward_block(features, first_weight, second_weight, vectors):
    width = features.shape[-1]
    normed = normalize(features.astype(jnp.float32), vectors).astype(jnp.bfloat16).reshape(-1, width)
    preact = jnp.dot(normed, first_weight, preferred_element_type=jnp.float32) + vectors[54:58].reshape(-1)
    activated = jax.nn.gelu(preact, approximate=False).astype(jnp.bfloat16)
    projected = jnp.dot(activated, second_weight, preferred_element_type=jnp.float32) + vectors[52]
    output = (features.astype(jnp.float32) + vectors[53] * projected.reshape(features.shape)).astype(jnp.bfloat16)
    return (output, normed, preact, activated, projected)

def backward_block(features, upstream, first_weight, second_weight, vectors, normed, preact, activated, projected):
    width = features.shape[-1]
    flat_up = upstream.astype(jnp.float32).reshape(-1, width)
    grad_scale = lax.optimization_barrier(jnp.sum(flat_up * projected, axis=0))
    dproj = flat_up * vectors[53]
    grad_bias_out = lax.optimization_barrier(jnp.sum(dproj, axis=0))
    dproj_b = dproj.astype(jnp.bfloat16)
    grad_second = lax.dot_general(activated, dproj_b, (((0,), (0,)), ((), ())), preferred_element_type=jnp.float32)
    dact = lax.dot_general(dproj_b, second_weight, (((1,), (1,)), ((), ())), preferred_element_type=jnp.float32)
    dpre = dact * gelu_slope(preact)
    grad_bias_in = lax.optimization_barrier(jnp.sum(dpre, axis=0))
    dpre_b = dpre.astype(jnp.bfloat16)
    grad_first = lax.dot_general(normed, dpre_b, (((0,), (0,)), ((), ())), preferred_element_type=jnp.float32)
    dnormed = lax.dot_general(dpre_b, first_weight, (((1,), (1,)), ((), ())), preferred_element_type=jnp.float32)
    unused, pullback = jax.vjp(normalize, features.astype(jnp.float32), vectors)
    grad_field, grad_small = pullback(dnormed.reshape(features.shape))
    grad_small = grad_small.at[52].add(grad_bias_out).at[53].add(grad_scale).at[54:58].add(grad_bias_in.reshape(4, width))
    down_grad = (grad_field + flat_up.reshape(features.shape)).astype(jnp.bfloat16)
    return (down_grad, grad_first, grad_second, grad_small)

def reference(inputs, out_grad, w_in, w_out, vector_params):
    sections = w_in.shape[0]
    sums_first = [jnp.zeros(w_in.shape[1:], jnp.float32) for index in range(sections)]
    sums_second = [jnp.zeros(w_out.shape[1:], jnp.float32) for index in range(sections)]
    sums_small = [jnp.zeros(vector_params.shape[1:], jnp.float32) for index in range(sections)]
    per_micro = []
    for micro_index in range(inputs.shape[0]):
        features = inputs[micro_index]
        kept = []
        for section in range(sections):
            kept.append(features)
            features = forward_block(features, w_in[section], w_out[section], vector_params[section])[0]
        upstream = out_grad[micro_index]
        segment_grads = [None] * sections
        for section in reversed(range(sections)):
            stash = forward_block(kept[section], w_in[section], w_out[section], vector_params[section])[1:]
            down_grad, grad_first, grad_second, grad_small = backward_block(kept[section], upstream, w_in[section], w_out[section], vector_params[section], *stash)
            sums_first[section] = sums_first[section] + grad_first
            sums_second[section] = sums_second[section] + grad_second
            sums_small[section] = sums_small[section] + grad_small
            segment_grads[section] = down_grad
            upstream = down_grad
        per_micro.append(jnp.stack(segment_grads))
    input_grads = jnp.stack(per_micro, axis=1)
    first_all = jnp.stack(sums_first)
    second_all = jnp.stack(sums_second)
    small_all = jnp.stack(sums_small)
    squares = jnp.sum(first_all * first_all) + jnp.sum(second_all * second_all) + jnp.sum(small_all * small_all)
    factor = jnp.minimum(1.0, jnp.sqrt(jnp.float32(PARAMS)) * lax.rsqrt(squares + 1e-06))
    return (input_grads, factor * first_all, factor * second_all, factor * small_all)
```

```python
import jax
import jax.numpy as jnp
from jax import lax
from jax.sharding import PartitionSpec as P


def from_behind(value, axis, by):
    devices = lax.axis_size(axis)
    pairs = [(i, i + by) for i in range(devices) if 0 <= i + by < devices]
    return lax.ppermute(value, axis, pairs)


def depthwise(features, vectors):
    height = features.shape[1]
    breadth = features.shape[2]
    padded = jnp.pad(features, ((0, 0), (3, 3), (3, 3), (0, 0)))
    summed = jnp.zeros(features.shape, jnp.float32)
    for row_shift in range(7):
        for col_shift in range(7):
            summed = (
                summed
                + padded[:, row_shift : row_shift + height, col_shift : col_shift + breadth, :]
                * vectors[row_shift * 7 + col_shift]
            )
    return summed + vectors[49]


def normalize(features, vectors):
    conv = depthwise(features, vectors)
    average = jnp.mean(conv, axis=-1, keepdims=True)
    centered = conv - average
    variance = jnp.mean(centered * centered, axis=-1, keepdims=True)
    return centered * lax.rsqrt(variance + 1e-06) * vectors[50] + vectors[51]


def gelu_slope(preact):
    cumulative = 0.5 * (1.0 + jax.scipy.special.erf(preact * 0.7071067811865476))
    return cumulative + preact * jnp.exp(-0.5 * preact * preact) * 0.3989422804014327


def forward_block(features, first_weight, second_weight, vectors):
    width = features.shape[-1]
    normed = (
        normalize(features.astype(jnp.float32), vectors).astype(jnp.bfloat16).reshape(-1, width)
    )
    preact = jnp.dot(normed, first_weight, preferred_element_type=jnp.float32) + vectors[
        54:58
    ].reshape(-1)
    activated = jax.nn.gelu(preact, approximate=False).astype(jnp.bfloat16)
    projected = jnp.dot(activated, second_weight, preferred_element_type=jnp.float32) + vectors[52]
    output = (
        features.astype(jnp.float32) + vectors[53] * projected.reshape(features.shape)
    ).astype(jnp.bfloat16)
    return (output, normed, preact, activated, projected)


def backward_block(
    features, upstream, first_weight, second_weight, vectors, normed, preact, activated, projected
):
    width = features.shape[-1]
    flat_up = upstream.astype(jnp.float32).reshape(-1, width)
    grad_scale = jnp.sum(flat_up * projected, axis=0)
    dproj = flat_up * vectors[53]
    grad_bias_out = jnp.sum(dproj, axis=0)
    dproj_b = dproj.astype(jnp.bfloat16)
    grad_second = lax.dot_general(
        activated, dproj_b, (((0,), (0,)), ((), ())), preferred_element_type=jnp.float32
    )
    dact = lax.dot_general(
        dproj_b, second_weight, (((1,), (1,)), ((), ())), preferred_element_type=jnp.float32
    )
    dpre = dact * gelu_slope(preact)
    grad_bias_in = jnp.sum(dpre, axis=0)
    dpre_b = dpre.astype(jnp.bfloat16)
    grad_first = lax.dot_general(
        normed, dpre_b, (((0,), (0,)), ((), ())), preferred_element_type=jnp.float32
    )
    dnormed = lax.dot_general(
        dpre_b, first_weight, (((1,), (1,)), ((), ())), preferred_element_type=jnp.float32
    )
    unused, pullback = jax.vjp(normalize, features.astype(jnp.float32), vectors)
    grad_field, grad_small = pullback(dnormed.reshape(features.shape))
    grad_small = (
        grad_small.at[52]
        .add(grad_bias_out)
        .at[53]
        .add(grad_scale)
        .at[54:58]
        .add(grad_bias_in.reshape(4, width))
    )
    down_grad = (grad_field + flat_up.reshape(features.shape)).astype(jnp.bfloat16)
    return (down_grad, grad_first, grad_second, grad_small)


def per_device(inputs, out_grad, w_in, w_out, vector_params):
    first_weight = w_in[0]
    second_weight = w_out[0]
    vectors = vector_params[0]
    section = lax.axis_index("segment")
    sections = lax.axis_size("segment")
    micro_count = inputs.shape[0]
    feature_shape = (micro_count * inputs.shape[1],) + inputs.shape[2:]
    batch_shape = inputs.shape
    width = feature_shape[-1]
    pixels = feature_shape[0] * feature_shape[1] * feature_shape[2]
    hidden = first_weight.shape[1]
    entering = inputs.reshape(feature_shape)
    leaving = out_grad.reshape(feature_shape)

    def run_forward(operands):
        features, stash = operands
        output, normed, preact, activated, projected = forward_block(
            features, first_weight, second_weight, vectors
        )
        return output, (features, normed, preact, activated, projected)

    def skip_forward(operands):
        features, stash = operands
        return jnp.zeros(feature_shape, jnp.bfloat16), stash

    stash = (
        jnp.zeros(feature_shape, jnp.bfloat16),
        jnp.zeros((pixels, width), jnp.bfloat16),
        jnp.zeros((pixels, hidden), jnp.float32),
        jnp.zeros((pixels, hidden), jnp.bfloat16),
        jnp.zeros((pixels, width), jnp.float32),
    )
    held = entering
    for tick_index in range(sections):
        output, stash = lax.cond(section == tick_index, run_forward, skip_forward, (held, stash))
        if tick_index + 1 < sections:
            held = from_behind(output, "segment", 1)

    def run_backward(operands):
        upstream, kept, grads = operands
        down_grad, grad_first, grad_second, grad_small = backward_block(
            stash[0], upstream, first_weight, second_weight, vectors, *stash[1:]
        )
        return down_grad, (grad_first, grad_second, grad_small)

    def skip_backward(operands):
        upstream, kept, grads = operands
        return kept, grads

    grads = (
        jnp.zeros(first_weight.shape, jnp.float32),
        jnp.zeros(second_weight.shape, jnp.float32),
        jnp.zeros(vectors.shape, jnp.float32),
    )
    kept = jnp.zeros(feature_shape, jnp.bfloat16)
    held = leaving
    for tick_index in range(sections):
        kept, grads = lax.cond(
            section == sections - 1 - tick_index, run_backward, skip_backward, (held, kept, grads)
        )
        if tick_index + 1 < sections:
            held = from_behind(kept, "segment", -1)
    acc_first, acc_second, acc_small = grads
    params_total = sections * (first_weight.size + second_weight.size + vectors.size)
    sum_first, sum_second, sum_small = lax.psum((acc_first, acc_second, acc_small), "dp")
    own_sum = (
        jnp.sum(sum_first * sum_first)
        + jnp.sum(sum_second * sum_second)
        + jnp.sum(sum_small * sum_small)
    )
    squares = lax.psum(own_sum, "segment")
    factor = jnp.minimum(1.0, jnp.sqrt(jnp.float32(params_total)) * lax.rsqrt(squares + 1e-06))
    step_first = factor * sum_first
    step_second = factor * sum_second
    step_small = factor * sum_small
    input_grads = kept.reshape(batch_shape)
    return (input_grads[None], step_first[None], step_second[None], step_small[None])


def solution(mesh):
    in_specs = (
        P(None, "dp", None, None, None),
        P(None, "dp", None, None, None),
        P("segment", None, None),
        P("segment", None, None),
        P("segment", None, None),
    )
    out_specs = (
        P("segment", None, "dp", None, None, None),
        P("segment", None, None),
        P("segment", None, None),
        P("segment", None, None),
    )
    return jax.shard_map(
        per_device, mesh=mesh, in_specs=in_specs, out_specs=out_specs, check_vma=False
    )
```

```python
import jax
import jax.numpy as jnp
from jax import lax
from jax.sharding import PartitionSpec as P


def from_behind(value, axis, by):
    devices = lax.axis_size(axis)
    pairs = [(i, i + by) for i in range(devices) if 0 <= i + by < devices]
    return lax.ppermute(value, axis, pairs)


def halving_reduce(parts, axis, orders):
    count = lax.axis_size(axis)
    me = lax.axis_index(axis)
    current = list(parts)
    for step in range(len(orders[0])):
        sides = []
        sends = []
        for index, piece in enumerate(current):
            bit = orders[index][step]
            side = (me >> bit) & 1
            halves = piece.reshape((2, piece.shape[0] // 2) + piece.shape[1:])
            sends.append(lax.dynamic_index_in_dim(halves, 1 - side, 0, keepdims=False))
            sides.append((side, halves))
        got = [
            lax.ppermute(send, axis, [(j, j ^ (1 << orders[index][step])) for j in range(count)])
            for index, send in enumerate(sends)
        ]
        current = [
            lax.dynamic_index_in_dim(halves, side, 0, keepdims=False) + received
            for (side, halves), received in zip(sides, got)
        ]
    return current


def doubling_gather(parts, axis, orders):
    count = lax.axis_size(axis)
    me = lax.axis_index(axis)
    current = list(parts)
    for step in reversed(range(len(orders[0]))):
        got = [
            lax.ppermute(piece, axis, [(j, j ^ (1 << orders[index][step])) for j in range(count)])
            for index, piece in enumerate(current)
        ]
        joined = []
        for index, (piece, received) in enumerate(zip(current, got)):
            side = (me >> orders[index][step]) & 1
            both = jnp.zeros((2,) + piece.shape, piece.dtype)
            both = lax.dynamic_update_index_in_dim(both, piece, side, 0)
            both = lax.dynamic_update_index_in_dim(both, received, 1 - side, 0)
            joined.append(both.reshape((2 * piece.shape[0],) + piece.shape[1:]))
        current = joined
    return current


def sum_over(arrays, axis):
    count = lax.axis_size(axis)
    bits = count.bit_length() - 1
    if count != 1 << bits or bits < 2:
        return lax.psum(tuple(arrays), axis)
    lanes = 128
    rows = [a.size // lanes for a in arrays]
    unit = 2 * count * 8
    total = -(-sum(rows) // unit) * unit
    flat = jnp.concatenate([a.reshape(-1, lanes) for a in arrays])
    flat = jnp.pad(flat, ((0, total - flat.shape[0]), (0, 0)))
    first = list(range(bits))
    second = [1, 0] + list(range(2, bits))
    halves = [flat[: total // 2], flat[total // 2 :]]
    shards = halving_reduce(halves, axis, (first, second))
    full = jnp.concatenate(doubling_gather(shards, axis, (first, second)))
    out = []
    offset = 0
    for a, r in zip(arrays, rows):
        out.append(full[offset : offset + r].reshape(a.shape))
        offset += r
    return tuple(out)


def depthwise(features, vectors):
    height = features.shape[1]
    breadth = features.shape[2]
    padded = jnp.pad(features, ((0, 0), (3, 3), (3, 3), (0, 0)))
    summed = jnp.zeros(features.shape, jnp.float32)
    for row_shift in range(7):
        for col_shift in range(7):
            summed = (
                summed
                + padded[:, row_shift : row_shift + height, col_shift : col_shift + breadth, :]
                * vectors[row_shift * 7 + col_shift]
            )
    return summed + vectors[49]


def normalize(features, vectors):
    conv = depthwise(features, vectors)
    average = jnp.mean(conv, axis=-1, keepdims=True)
    centered = conv - average
    variance = jnp.mean(centered * centered, axis=-1, keepdims=True)
    return centered * lax.rsqrt(variance + 1e-06) * vectors[50] + vectors[51]


def gelu_slope(preact):
    cumulative = 0.5 * (1.0 + jax.scipy.special.erf(preact * 0.7071067811865476))
    return cumulative + preact * jnp.exp(-0.5 * preact * preact) * 0.3989422804014327


def forward_block(features, first_weight, second_weight, vectors):
    width = features.shape[-1]
    normed = (
        normalize(features.astype(jnp.float32), vectors).astype(jnp.bfloat16).reshape(-1, width)
    )
    preact = jnp.dot(normed, first_weight, preferred_element_type=jnp.float32) + vectors[
        54:58
    ].reshape(-1)
    activated = jax.nn.gelu(preact, approximate=False).astype(jnp.bfloat16)
    projected = jnp.dot(activated, second_weight, preferred_element_type=jnp.float32) + vectors[52]
    output = (
        features.astype(jnp.float32) + vectors[53] * projected.reshape(features.shape)
    ).astype(jnp.bfloat16)
    return (output, normed, preact, activated, projected)


def backward_block(
    features, upstream, first_weight, second_weight, vectors, normed, preact, activated, projected
):
    width = features.shape[-1]
    flat_up = upstream.astype(jnp.float32).reshape(-1, width)
    grad_scale = jnp.sum(flat_up * projected, axis=0)
    dproj = flat_up * vectors[53]
    grad_bias_out = jnp.sum(dproj, axis=0)
    dproj_b = dproj.astype(jnp.bfloat16)
    grad_second = lax.dot_general(
        activated, dproj_b, (((0,), (0,)), ((), ())), preferred_element_type=jnp.float32
    )
    dact = lax.dot_general(
        dproj_b, second_weight, (((1,), (1,)), ((), ())), preferred_element_type=jnp.float32
    )
    dpre = dact * gelu_slope(preact)
    grad_bias_in = jnp.sum(dpre, axis=0)
    dpre_b = dpre.astype(jnp.bfloat16)
    grad_first = lax.dot_general(
        normed, dpre_b, (((0,), (0,)), ((), ())), preferred_element_type=jnp.float32
    )
    dnormed = lax.dot_general(
        dpre_b, first_weight, (((1,), (1,)), ((), ())), preferred_element_type=jnp.float32
    )
    unused, pullback = jax.vjp(normalize, features.astype(jnp.float32), vectors)
    grad_field, grad_small = pullback(dnormed.reshape(features.shape))
    grad_small = (
        grad_small.at[52]
        .add(grad_bias_out)
        .at[53]
        .add(grad_scale)
        .at[54:58]
        .add(grad_bias_in.reshape(4, width))
    )
    down_grad = (grad_field + flat_up.reshape(features.shape)).astype(jnp.bfloat16)
    return (down_grad, grad_first, grad_second, grad_small)


def per_device(inputs, out_grad, w_in, w_out, vector_params):
    first_weight = w_in[0]
    second_weight = w_out[0]
    vectors = vector_params[0]
    section = lax.axis_index("segment")
    sections = lax.axis_size("segment")
    micro_count = inputs.shape[0]
    feature_shape = (micro_count * inputs.shape[1],) + inputs.shape[2:]
    batch_shape = inputs.shape
    width = feature_shape[-1]
    pixels = feature_shape[0] * feature_shape[1] * feature_shape[2]
    hidden = first_weight.shape[1]
    entering = inputs.reshape(feature_shape)
    leaving = out_grad.reshape(feature_shape)

    def run_forward(operands):
        features, stash = operands
        output, normed, preact, activated, projected = forward_block(
            features, first_weight, second_weight, vectors
        )
        return output, (features, normed, preact, activated, projected)

    def skip_forward(operands):
        features, stash = operands
        return jnp.zeros(feature_shape, jnp.bfloat16), stash

    stash = (
        jnp.zeros(feature_shape, jnp.bfloat16),
        jnp.zeros((pixels, width), jnp.bfloat16),
        jnp.zeros((pixels, hidden), jnp.float32),
        jnp.zeros((pixels, hidden), jnp.bfloat16),
        jnp.zeros((pixels, width), jnp.float32),
    )
    held = entering
    for tick_index in range(sections):
        output, stash = lax.cond(section == tick_index, run_forward, skip_forward, (held, stash))
        if tick_index + 1 < sections:
            held = from_behind(output, "segment", 1)

    def run_backward(operands):
        upstream, kept, grads = operands
        down_grad, grad_first, grad_second, grad_small = backward_block(
            stash[0], upstream, first_weight, second_weight, vectors, *stash[1:]
        )
        return down_grad, (grad_first, grad_second, grad_small)

    def skip_backward(operands):
        upstream, kept, grads = operands
        return kept, grads

    grads = (
        jnp.zeros(first_weight.shape, jnp.float32),
        jnp.zeros(second_weight.shape, jnp.float32),
        jnp.zeros(vectors.shape, jnp.float32),
    )
    kept = jnp.zeros(feature_shape, jnp.bfloat16)
    held = leaving
    for tick_index in range(sections):
        kept, grads = lax.cond(
            section == sections - 1 - tick_index, run_backward, skip_backward, (held, kept, grads)
        )
        if tick_index + 1 < sections:
            held = from_behind(kept, "segment", -1)
    acc_first, acc_second, acc_small = grads
    params_total = sections * (first_weight.size + second_weight.size + vectors.size)
    sum_first, sum_second, sum_small = sum_over((acc_first, acc_second, acc_small), "dp")
    own_sum = (
        jnp.sum(sum_first * sum_first)
        + jnp.sum(sum_second * sum_second)
        + jnp.sum(sum_small * sum_small)
    )
    squares = lax.psum(own_sum, "segment")
    factor = jnp.minimum(1.0, jnp.sqrt(jnp.float32(params_total)) * lax.rsqrt(squares + 1e-06))
    step_first = factor * sum_first
    step_second = factor * sum_second
    step_small = factor * sum_small
    input_grads = kept.reshape(batch_shape)
    return (input_grads[None], step_first[None], step_second[None], step_small[None])


def solution(mesh):
    in_specs = (
        P(None, "dp", None, None, None),
        P(None, "dp", None, None, None),
        P("segment", None, None),
        P("segment", None, None),
        P("segment", None, None),
    )
    out_specs = (
        P("segment", None, "dp", None, None, None),
        P("segment", None, None),
        P("segment", None, None),
        P("segment", None, None),
    )
    return jax.shard_map(
        per_device, mesh=mesh, in_specs=in_specs, out_specs=out_specs, check_vma=False
    )
```

```python
import jax
import jax.numpy as jnp
from jax import lax
from jax.sharding import PartitionSpec as P


def from_behind(value, axis, by):
    devices = lax.axis_size(axis)
    pairs = [(i, i + by) for i in range(devices) if 0 <= i + by < devices]
    return lax.ppermute(value, axis, pairs)


def halving_reduce(parts, axis, orders):
    count = lax.axis_size(axis)
    me = lax.axis_index(axis)
    current = list(parts)
    for step in range(len(orders[0])):
        sides = []
        sends = []
        for index, piece in enumerate(current):
            bit = orders[index][step]
            side = (me >> bit) & 1
            halves = piece.reshape((2, piece.shape[0] // 2) + piece.shape[1:])
            sends.append(lax.dynamic_index_in_dim(halves, 1 - side, 0, keepdims=False))
            sides.append((side, halves))
        got = [
            lax.ppermute(send, axis, [(j, j ^ (1 << orders[index][step])) for j in range(count)])
            for index, send in enumerate(sends)
        ]
        current = [
            lax.dynamic_index_in_dim(halves, side, 0, keepdims=False) + received
            for (side, halves), received in zip(sides, got)
        ]
    return current


def doubling_gather(parts, axis, orders):
    count = lax.axis_size(axis)
    me = lax.axis_index(axis)
    current = list(parts)
    for step in reversed(range(len(orders[0]))):
        got = [
            lax.ppermute(piece, axis, [(j, j ^ (1 << orders[index][step])) for j in range(count)])
            for index, piece in enumerate(current)
        ]
        joined = []
        for index, (piece, received) in enumerate(zip(current, got)):
            side = (me >> orders[index][step]) & 1
            both = jnp.zeros((2,) + piece.shape, piece.dtype)
            both = lax.dynamic_update_index_in_dim(both, piece, side, 0)
            both = lax.dynamic_update_index_in_dim(both, received, 1 - side, 0)
            joined.append(both.reshape((2 * piece.shape[0],) + piece.shape[1:]))
        current = joined
    return current


def sum_over(arrays, axis):
    count = lax.axis_size(axis)
    bits = count.bit_length() - 1
    if count != 1 << bits or bits < 2:
        return lax.psum(tuple(arrays), axis)
    first_grad, second_grad, small_grad = arrays
    rows = second_grad.shape[0] + small_grad.shape[0]
    unit = 8 * count
    total = -(-rows // unit) * unit
    joined = jnp.concatenate(
        [second_grad, small_grad, jnp.zeros((total - rows, small_grad.shape[1]), small_grad.dtype)]
    )
    orders = (list(range(bits)), [1, 0] + list(range(2, bits)))
    shards = halving_reduce([first_grad, joined], axis, orders)
    first_sum, joined_sum = doubling_gather(shards, axis, orders)
    second_rows = second_grad.shape[0]
    return (
        first_sum,
        joined_sum[:second_rows],
        joined_sum[second_rows : second_rows + small_grad.shape[0]],
    )


def depthwise(features, vectors):
    height = features.shape[1]
    breadth = features.shape[2]
    padded = jnp.pad(features, ((0, 0), (3, 3), (3, 3), (0, 0)))
    summed = jnp.zeros(features.shape, jnp.float32)
    for row_shift in range(7):
        for col_shift in range(7):
            summed = (
                summed
                + padded[:, row_shift : row_shift + height, col_shift : col_shift + breadth, :]
                * vectors[row_shift * 7 + col_shift]
            )
    return summed + vectors[49]


def normalize(features, vectors):
    conv = depthwise(features, vectors)
    average = jnp.mean(conv, axis=-1, keepdims=True)
    centered = conv - average
    variance = jnp.mean(centered * centered, axis=-1, keepdims=True)
    return centered * lax.rsqrt(variance + 1e-06) * vectors[50] + vectors[51]


def gelu_slope(preact):
    cumulative = 0.5 * (1.0 + jax.scipy.special.erf(preact * 0.7071067811865476))
    return cumulative + preact * jnp.exp(-0.5 * preact * preact) * 0.3989422804014327


def forward_block(features, first_weight, second_weight, vectors):
    width = features.shape[-1]
    normed = (
        normalize(features.astype(jnp.float32), vectors).astype(jnp.bfloat16).reshape(-1, width)
    )
    preact = jnp.dot(normed, first_weight, preferred_element_type=jnp.float32) + vectors[
        54:58
    ].reshape(-1)
    activated = jax.nn.gelu(preact, approximate=False).astype(jnp.bfloat16)
    projected = jnp.dot(activated, second_weight, preferred_element_type=jnp.float32) + vectors[52]
    output = (
        features.astype(jnp.float32) + vectors[53] * projected.reshape(features.shape)
    ).astype(jnp.bfloat16)
    return (output, normed, preact, activated, projected)


def backward_block(
    features, upstream, first_weight, second_weight, vectors, normed, preact, activated, projected
):
    width = features.shape[-1]
    flat_up = upstream.astype(jnp.float32).reshape(-1, width)
    grad_scale = jnp.sum(flat_up * projected, axis=0)
    dproj = flat_up * vectors[53]
    grad_bias_out = jnp.sum(dproj, axis=0)
    dproj_b = dproj.astype(jnp.bfloat16)
    grad_second = lax.dot_general(
        activated, dproj_b, (((0,), (0,)), ((), ())), preferred_element_type=jnp.float32
    )
    dact = lax.dot_general(
        dproj_b, second_weight, (((1,), (1,)), ((), ())), preferred_element_type=jnp.float32
    )
    dpre = dact * gelu_slope(preact)
    grad_bias_in = jnp.sum(dpre, axis=0)
    dpre_b = dpre.astype(jnp.bfloat16)
    grad_first = lax.dot_general(
        normed, dpre_b, (((0,), (0,)), ((), ())), preferred_element_type=jnp.float32
    )
    dnormed = lax.dot_general(
        dpre_b, first_weight, (((1,), (1,)), ((), ())), preferred_element_type=jnp.float32
    )
    unused, pullback = jax.vjp(normalize, features.astype(jnp.float32), vectors)
    grad_field, grad_small = pullback(dnormed.reshape(features.shape))
    grad_small = jnp.concatenate(
        [
            grad_small[:52],
            grad_small[52:53] + grad_bias_out[None],
            grad_small[53:54] + grad_scale[None],
            grad_small[54:58] + grad_bias_in.reshape(4, width),
        ]
    )
    down_grad = (grad_field + flat_up.reshape(features.shape)).astype(jnp.bfloat16)
    return (down_grad, grad_first, grad_second, grad_small)


def per_device(inputs, out_grad, w_in, w_out, vector_params):
    first_weight = w_in[0]
    second_weight = w_out[0]
    vectors = vector_params[0]
    section = lax.axis_index("segment")
    sections = lax.axis_size("segment")
    micro_count = inputs.shape[0]
    feature_shape = (micro_count * inputs.shape[1],) + inputs.shape[2:]
    batch_shape = inputs.shape
    width = feature_shape[-1]
    pixels = feature_shape[0] * feature_shape[1] * feature_shape[2]
    hidden = first_weight.shape[1]
    entering = inputs.reshape(feature_shape)
    leaving = out_grad.reshape(feature_shape)

    def run_forward(operands):
        features, stash = operands
        output, normed, preact, activated, projected = forward_block(
            features, first_weight, second_weight, vectors
        )
        return output, (features, normed, preact, activated, projected)

    def skip_forward(operands):
        features, stash = operands
        return jnp.zeros(feature_shape, jnp.bfloat16), stash

    stash = (
        jnp.zeros(feature_shape, jnp.bfloat16),
        jnp.zeros((pixels, width), jnp.bfloat16),
        jnp.zeros((pixels, hidden), jnp.float32),
        jnp.zeros((pixels, hidden), jnp.bfloat16),
        jnp.zeros((pixels, width), jnp.float32),
    )
    held = entering
    for tick_index in range(sections):
        output, stash = lax.cond(section == tick_index, run_forward, skip_forward, (held, stash))
        if tick_index + 1 < sections:
            held = from_behind(output, "segment", 1)

    def run_backward(operands):
        upstream, kept, grads = operands
        down_grad, grad_first, grad_second, grad_small = backward_block(
            stash[0], upstream, first_weight, second_weight, vectors, *stash[1:]
        )
        return down_grad, (grad_first, grad_second, grad_small)

    def skip_backward(operands):
        upstream, kept, grads = operands
        return kept, grads

    grads = (
        jnp.zeros(first_weight.shape, jnp.float32),
        jnp.zeros(second_weight.shape, jnp.float32),
        jnp.zeros(vectors.shape, jnp.float32),
    )
    kept = jnp.zeros(feature_shape, jnp.bfloat16)
    held = leaving
    for tick_index in range(sections):
        kept, grads = lax.cond(
            section == sections - 1 - tick_index, run_backward, skip_backward, (held, kept, grads)
        )
        if tick_index + 1 < sections:
            held = from_behind(kept, "segment", -1)
    acc_first, acc_second, acc_small = grads
    params_total = sections * (first_weight.size + second_weight.size + vectors.size)
    sum_first, sum_second, sum_small = sum_over((acc_first, acc_second, acc_small), "dp")
    own_sum = (
        jnp.sum(sum_first * sum_first)
        + jnp.sum(sum_second * sum_second)
        + jnp.sum(sum_small * sum_small)
    )
    squares = lax.psum(own_sum, "segment")
    factor = jnp.minimum(1.0, jnp.sqrt(jnp.float32(params_total)) * lax.rsqrt(squares + 1e-06))
    step_first = factor * sum_first
    step_second = factor * sum_second
    step_small = factor * sum_small
    input_grads = kept.reshape(batch_shape)
    return (input_grads[None], step_first[None], step_second[None], step_small[None])


def solution(mesh):
    in_specs = (
        P(None, "dp", None, None, None),
        P(None, "dp", None, None, None),
        P("segment", None, None),
        P("segment", None, None),
        P("segment", None, None),
    )
    out_specs = (
        P("segment", None, "dp", None, None, None),
        P("segment", None, None),
        P("segment", None, None),
        P("segment", None, None),
    )
    return jax.shard_map(
        per_device, mesh=mesh, in_specs=in_specs, out_specs=out_specs, check_vma=False
    )
```

```python
import jax
import jax.numpy as jnp
from jax import lax
from jax.sharding import PartitionSpec as P


def from_behind(value, axis, by):
    devices = lax.axis_size(axis)
    pairs = [(i, i + by) for i in range(devices) if 0 <= i + by < devices]
    return lax.ppermute(value, axis, pairs)


def halving_reduce(parts, axis, orders):
    count = lax.axis_size(axis)
    me = lax.axis_index(axis)
    current = list(parts)
    for step in range(len(orders[0])):
        sides = []
        sends = []
        for index, piece in enumerate(current):
            bit = orders[index][step]
            side = (me >> bit) & 1
            halves = piece.reshape((2, piece.shape[0] // 2) + piece.shape[1:])
            sends.append(lax.dynamic_index_in_dim(halves, 1 - side, 0, keepdims=False))
            sides.append((side, halves))
        got = [
            lax.ppermute(send, axis, [(j, j ^ (1 << orders[index][step])) for j in range(count)])
            for index, send in enumerate(sends)
        ]
        current = [
            lax.dynamic_index_in_dim(halves, side, 0, keepdims=False) + received
            for (side, halves), received in zip(sides, got)
        ]
    return current


def doubling_gather(parts, axis, orders):
    count = lax.axis_size(axis)
    me = lax.axis_index(axis)
    current = list(parts)
    for step in reversed(range(len(orders[0]))):
        got = [
            lax.ppermute(piece, axis, [(j, j ^ (1 << orders[index][step])) for j in range(count)])
            for index, piece in enumerate(current)
        ]
        joined = []
        for index, (piece, received) in enumerate(zip(current, got)):
            side = (me >> orders[index][step]) & 1
            both = jnp.zeros((2,) + piece.shape, piece.dtype)
            both = lax.dynamic_update_index_in_dim(both, piece, side, 0)
            both = lax.dynamic_update_index_in_dim(both, received, 1 - side, 0)
            joined.append(both.reshape((2 * piece.shape[0],) + piece.shape[1:]))
        current = joined
    return current


def sum_over(arrays, axis):
    count = lax.axis_size(axis)
    bits = count.bit_length() - 1
    if count != 1 << bits or bits < 2:
        sums = lax.psum(tuple(arrays), axis)
        return sums, sum(jnp.sum(s * s) for s in sums)
    first_grad, second_grad, small_grad = arrays
    rows = second_grad.shape[0] + small_grad.shape[0]
    unit = 8 * count
    total = -(-rows // unit) * unit
    joined = jnp.concatenate(
        [second_grad, small_grad, jnp.zeros((total - rows, small_grad.shape[1]), small_grad.dtype)]
    )
    orders = (list(range(bits)), [1, 0] + list(range(2, bits)))
    shards = halving_reduce([first_grad, joined], axis, orders)
    own = sum(jnp.sum(s * s) for s in shards)
    tile = jnp.broadcast_to(own, (1, 128)).astype(jnp.float32)
    narrow = [s.astype(jnp.bfloat16) for s in shards]
    first_sum, joined_sum, squares = doubling_gather(narrow + [tile], axis, orders + (orders[0],))
    second_rows = second_grad.shape[0]
    sums = (
        first_sum.astype(jnp.float32),
        joined_sum[:second_rows].astype(jnp.float32),
        joined_sum[second_rows : second_rows + small_grad.shape[0]].astype(jnp.float32),
    )
    return sums, jnp.sum(squares[:, 0])


def depthwise(features, vectors):
    height = features.shape[1]
    breadth = features.shape[2]
    padded = jnp.pad(features, ((0, 0), (3, 3), (3, 3), (0, 0)))
    summed = jnp.zeros(features.shape, jnp.float32)
    for row_shift in range(7):
        for col_shift in range(7):
            summed = (
                summed
                + padded[:, row_shift : row_shift + height, col_shift : col_shift + breadth, :]
                * vectors[row_shift * 7 + col_shift]
            )
    return summed + vectors[49]


def normalize(features, vectors):
    conv = depthwise(features, vectors)
    average = jnp.mean(conv, axis=-1, keepdims=True)
    centered = conv - average
    variance = jnp.mean(centered * centered, axis=-1, keepdims=True)
    return centered * lax.rsqrt(variance + 1e-06) * vectors[50] + vectors[51]


def gelu_slope(preact):
    cumulative = 0.5 * (1.0 + jax.scipy.special.erf(preact * 0.7071067811865476))
    return cumulative + preact * jnp.exp(-0.5 * preact * preact) * 0.3989422804014327


def forward_block(features, first_weight, second_weight, vectors):
    width = features.shape[-1]
    normed = (
        normalize(features.astype(jnp.float32), vectors).astype(jnp.bfloat16).reshape(-1, width)
    )
    preact = jnp.dot(normed, first_weight, preferred_element_type=jnp.float32) + vectors[
        54:58
    ].reshape(-1)
    activated = jax.nn.gelu(preact, approximate=False).astype(jnp.bfloat16)
    projected = jnp.dot(activated, second_weight, preferred_element_type=jnp.float32) + vectors[52]
    output = (
        features.astype(jnp.float32) + vectors[53] * projected.reshape(features.shape)
    ).astype(jnp.bfloat16)
    return (output, normed, preact, activated, projected)


def backward_block(
    features, upstream, first_weight, second_weight, vectors, normed, preact, activated, projected
):
    width = features.shape[-1]
    flat_up = upstream.astype(jnp.float32).reshape(-1, width)
    grad_scale = jnp.sum(flat_up * projected, axis=0)
    dproj = flat_up * vectors[53]
    grad_bias_out = jnp.sum(dproj, axis=0)
    dproj_b = dproj.astype(jnp.bfloat16)
    grad_second = lax.dot_general(
        activated, dproj_b, (((0,), (0,)), ((), ())), preferred_element_type=jnp.float32
    )
    dact = lax.dot_general(
        dproj_b, second_weight, (((1,), (1,)), ((), ())), preferred_element_type=jnp.float32
    )
    dpre = dact * gelu_slope(preact)
    grad_bias_in = jnp.sum(dpre, axis=0)
    dpre_b = dpre.astype(jnp.bfloat16)
    grad_first = lax.dot_general(
        normed, dpre_b, (((0,), (0,)), ((), ())), preferred_element_type=jnp.float32
    )
    dnormed = lax.dot_general(
        dpre_b, first_weight, (((1,), (1,)), ((), ())), preferred_element_type=jnp.float32
    )
    unused, pullback = jax.vjp(normalize, features.astype(jnp.float32), vectors)
    grad_field, grad_small = pullback(dnormed.reshape(features.shape))
    grad_small = jnp.concatenate(
        [
            grad_small[:52],
            grad_small[52:53] + grad_bias_out[None],
            grad_small[53:54] + grad_scale[None],
            grad_small[54:58] + grad_bias_in.reshape(4, width),
        ]
    )
    down_grad = (grad_field + flat_up.reshape(features.shape)).astype(jnp.bfloat16)
    return (down_grad, grad_first, grad_second, grad_small)


def per_device(inputs, out_grad, w_in, w_out, vector_params):
    first_weight = w_in[0]
    second_weight = w_out[0]
    vectors = vector_params[0]
    section = lax.axis_index("segment")
    sections = lax.axis_size("segment")
    micro_count = inputs.shape[0]
    feature_shape = (micro_count * inputs.shape[1],) + inputs.shape[2:]
    batch_shape = inputs.shape
    width = feature_shape[-1]
    pixels = feature_shape[0] * feature_shape[1] * feature_shape[2]
    hidden = first_weight.shape[1]
    entering = inputs.reshape(feature_shape)
    leaving = out_grad.reshape(feature_shape)

    def run_forward(operands):
        features, stash = operands
        output, normed, preact, activated, projected = forward_block(
            features, first_weight, second_weight, vectors
        )
        return output, (features, normed, preact, activated, projected)

    def skip_forward(operands):
        features, stash = operands
        return jnp.zeros(feature_shape, jnp.bfloat16), stash

    stash = (
        jnp.zeros(feature_shape, jnp.bfloat16),
        jnp.zeros((pixels, width), jnp.bfloat16),
        jnp.zeros((pixels, hidden), jnp.float32),
        jnp.zeros((pixels, hidden), jnp.bfloat16),
        jnp.zeros((pixels, width), jnp.float32),
    )
    held = entering
    for tick_index in range(sections):
        output, stash = lax.cond(section == tick_index, run_forward, skip_forward, (held, stash))
        if tick_index + 1 < sections:
            held = from_behind(output, "segment", 1)

    def run_backward(operands):
        upstream, kept, grads = operands
        down_grad, grad_first, grad_second, grad_small = backward_block(
            stash[0], upstream, first_weight, second_weight, vectors, *stash[1:]
        )
        return down_grad, (grad_first, grad_second, grad_small)

    def skip_backward(operands):
        upstream, kept, grads = operands
        return kept, grads

    grads = (
        jnp.zeros(first_weight.shape, jnp.float32),
        jnp.zeros(second_weight.shape, jnp.float32),
        jnp.zeros(vectors.shape, jnp.float32),
    )
    kept = jnp.zeros(feature_shape, jnp.bfloat16)
    held = leaving
    for tick_index in range(sections):
        kept, grads = lax.cond(
            section == sections - 1 - tick_index, run_backward, skip_backward, (held, kept, grads)
        )
        if tick_index + 1 < sections:
            held = from_behind(kept, "segment", -1)
    acc_first, acc_second, acc_small = grads
    params_total = sections * (first_weight.size + second_weight.size + vectors.size)
    (sum_first, sum_second, sum_small), own_sum = sum_over((acc_first, acc_second, acc_small), "dp")
    squares = lax.psum(own_sum, "segment")
    factor = jnp.minimum(1.0, jnp.sqrt(jnp.float32(params_total)) * lax.rsqrt(squares + 1e-06))
    step_first = factor * sum_first
    step_second = factor * sum_second
    step_small = factor * sum_small
    input_grads = kept.reshape(batch_shape)
    return (input_grads[None], step_first[None], step_second[None], step_small[None])


def solution(mesh):
    in_specs = (
        P(None, "dp", None, None, None),
        P(None, "dp", None, None, None),
        P("segment", None, None),
        P("segment", None, None),
        P("segment", None, None),
    )
    out_specs = (
        P("segment", None, "dp", None, None, None),
        P("segment", None, None),
        P("segment", None, None),
        P("segment", None, None),
    )
    return jax.shard_map(
        per_device, mesh=mesh, in_specs=in_specs, out_specs=out_specs, check_vma=False
    )
```

```python
import jax
import jax.numpy as jnp
from jax import lax
from jax.sharding import PartitionSpec as P


def from_behind(value, axis, by):
    devices = lax.axis_size(axis)
    pairs = [(i, i + by) for i in range(devices) if 0 <= i + by < devices]
    return lax.ppermute(value, axis, pairs)


def halving_reduce(parts, axis, orders):
    count = lax.axis_size(axis)
    me = lax.axis_index(axis)
    current = list(parts)
    for step in range(len(orders[0])):
        sides = []
        sends = []
        for index, piece in enumerate(current):
            bit = orders[index][step]
            side = (me >> bit) & 1
            halves = piece.reshape((2, piece.shape[0] // 2) + piece.shape[1:])
            sends.append(lax.dynamic_index_in_dim(halves, 1 - side, 0, keepdims=False))
            sides.append((side, halves))
        got = [
            lax.ppermute(send, axis, [(j, j ^ (1 << orders[index][step])) for j in range(count)])
            for index, send in enumerate(sends)
        ]
        current = [
            lax.dynamic_index_in_dim(halves, side, 0, keepdims=False) + received
            for (side, halves), received in zip(sides, got)
        ]
    return current


def doubling_gather(parts, axis, orders):
    count = lax.axis_size(axis)
    me = lax.axis_index(axis)
    current = list(parts)
    for step in reversed(range(len(orders[0]))):
        got = [
            lax.ppermute(piece, axis, [(j, j ^ (1 << orders[index][step])) for j in range(count)])
            for index, piece in enumerate(current)
        ]
        joined = []
        for index, (piece, received) in enumerate(zip(current, got)):
            side = (me >> orders[index][step]) & 1
            both = jnp.zeros((2,) + piece.shape, piece.dtype)
            both = lax.dynamic_update_index_in_dim(both, piece, side, 0)
            both = lax.dynamic_update_index_in_dim(both, received, 1 - side, 0)
            joined.append(both.reshape((2 * piece.shape[0],) + piece.shape[1:]))
        current = joined
    return current


def sum_over(arrays, axis):
    count = lax.axis_size(axis)
    bits = count.bit_length() - 1
    if count != 1 << bits or bits < 2:
        return lax.psum(tuple(arrays), axis)
    first_grad, second_grad, small_grad = arrays
    rows = second_grad.shape[0] + small_grad.shape[0]
    unit = 8 * count
    total = -(-rows // unit) * unit
    joined = jnp.concatenate(
        [second_grad, small_grad, jnp.zeros((total - rows, small_grad.shape[1]), small_grad.dtype)]
    )
    orders = (list(range(bits)), [1, 0] + list(range(2, bits)))
    shards = halving_reduce([first_grad, joined], axis, orders)
    first_sum, joined_sum = doubling_gather(shards, axis, orders)
    second_rows = second_grad.shape[0]
    return (
        first_sum,
        joined_sum[:second_rows],
        joined_sum[second_rows : second_rows + small_grad.shape[0]],
    )


def depthwise(features, vectors):
    height = features.shape[1]
    breadth = features.shape[2]
    padded = jnp.pad(features, ((0, 0), (3, 3), (3, 3), (0, 0)))
    summed = jnp.zeros(features.shape, jnp.float32)
    for row_shift in range(7):
        for col_shift in range(7):
            summed = (
                summed
                + padded[:, row_shift : row_shift + height, col_shift : col_shift + breadth, :]
                * vectors[row_shift * 7 + col_shift]
            )
    return summed + vectors[49]


def normalize(features, vectors):
    conv = depthwise(features, vectors)
    average = jnp.mean(conv, axis=-1, keepdims=True)
    centered = conv - average
    variance = jnp.mean(centered * centered, axis=-1, keepdims=True)
    return centered * lax.rsqrt(variance + 1e-06) * vectors[50] + vectors[51]


def gelu_slope(preact):
    cumulative = 0.5 * (1.0 + jax.scipy.special.erf(preact * 0.7071067811865476))
    return cumulative + preact * jnp.exp(-0.5 * preact * preact) * 0.3989422804014327


def forward_block(features, first_weight, second_weight, vectors):
    width = features.shape[-1]
    normed = (
        normalize(features.astype(jnp.float32), vectors).astype(jnp.bfloat16).reshape(-1, width)
    )
    preact = jnp.dot(normed, first_weight, preferred_element_type=jnp.float32) + vectors[
        54:58
    ].reshape(-1)
    activated = jax.nn.gelu(preact, approximate=False).astype(jnp.bfloat16)
    projected = jnp.dot(activated, second_weight, preferred_element_type=jnp.float32) + vectors[52]
    output = (
        features.astype(jnp.float32) + vectors[53] * projected.reshape(features.shape)
    ).astype(jnp.bfloat16)
    return (output, normed, preact, activated, projected)


def backward_block(
    features, upstream, first_weight, second_weight, vectors, normed, preact, activated, projected
):
    width = features.shape[-1]
    flat_up = upstream.astype(jnp.float32).reshape(-1, width)
    grad_scale = jnp.sum(flat_up * projected, axis=0)
    dproj = flat_up * vectors[53]
    grad_bias_out = jnp.sum(dproj, axis=0)
    dproj_b = dproj.astype(jnp.bfloat16)
    grad_second = lax.dot_general(
        activated, dproj_b, (((0,), (0,)), ((), ())), preferred_element_type=jnp.float32
    )
    dact = lax.dot_general(
        dproj_b, second_weight, (((1,), (1,)), ((), ())), preferred_element_type=jnp.float32
    )
    dpre = dact * gelu_slope(preact)
    grad_bias_in = jnp.sum(dpre, axis=0)
    dpre_b = dpre.astype(jnp.bfloat16)
    grad_first = lax.dot_general(
        normed, dpre_b, (((0,), (0,)), ((), ())), preferred_element_type=jnp.float32
    )
    dnormed = lax.dot_general(
        dpre_b, first_weight, (((1,), (1,)), ((), ())), preferred_element_type=jnp.float32
    )
    unused, pullback = jax.vjp(normalize, features.astype(jnp.float32), vectors)
    grad_field, grad_small = pullback(dnormed.reshape(features.shape))
    grad_small = jnp.concatenate(
        [
            grad_small[:52],
            grad_small[52:53] + grad_bias_out[None],
            grad_small[53:54] + grad_scale[None],
            grad_small[54:58] + grad_bias_in.reshape(4, width),
        ]
    )
    down_grad = (grad_field + flat_up.reshape(features.shape)).astype(jnp.bfloat16)
    return (down_grad, grad_first, grad_second, grad_small)


def per_device(inputs, out_grad, w_in, w_out, vector_params):
    first_weight = w_in[0]
    second_weight = w_out[0]
    vectors = vector_params[0]
    section = lax.axis_index("segment")
    sections = lax.axis_size("segment")
    micro_count = inputs.shape[0]
    feature_shape = (micro_count * inputs.shape[1],) + inputs.shape[2:]
    batch_shape = inputs.shape
    width = feature_shape[-1]
    pixels = feature_shape[0] * feature_shape[1] * feature_shape[2]
    hidden = first_weight.shape[1]
    entering = inputs.reshape(feature_shape)
    leaving = out_grad.reshape(feature_shape)

    def run_forward(operands):
        features, stash = operands
        output, normed, preact, activated, projected = forward_block(
            features, first_weight, second_weight, vectors
        )
        return output, (features, normed, preact, activated, projected)

    def skip_forward(operands):
        features, stash = operands
        return jnp.zeros(feature_shape, jnp.bfloat16), stash

    stash = (
        jnp.zeros(feature_shape, jnp.bfloat16),
        jnp.zeros((pixels, width), jnp.bfloat16),
        jnp.zeros((pixels, hidden), jnp.float32),
        jnp.zeros((pixels, hidden), jnp.bfloat16),
        jnp.zeros((pixels, width), jnp.float32),
    )
    held = entering
    for tick_index in range(sections):
        output, stash = lax.cond(section == tick_index, run_forward, skip_forward, (held, stash))
        if tick_index + 1 < sections:
            held = from_behind(output, "segment", 1)

    features, normed, preact, activated, projected = stash

    def run_head(operands):
        upstream, kept = operands
        flat_up = upstream.astype(jnp.float32).reshape(-1, width)
        grad_scale = jnp.sum(flat_up * projected, axis=0)
        dproj = flat_up * vectors[53]
        grad_bias_out = jnp.sum(dproj, axis=0)
        dproj_b = dproj.astype(jnp.bfloat16)
        dact = lax.dot_general(
            dproj_b, second_weight, (((1,), (1,)), ((), ())), preferred_element_type=jnp.float32
        )
        dpre = dact * gelu_slope(preact)
        grad_bias_in = jnp.sum(dpre, axis=0)
        dpre_b = dpre.astype(jnp.bfloat16)
        dnormed = lax.dot_general(
            dpre_b, first_weight, (((1,), (1,)), ((), ())), preferred_element_type=jnp.float32
        )
        return (dproj_b, dpre_b, dnormed, grad_scale, grad_bias_out, grad_bias_in)

    def skip_head(operands):
        upstream, kept = operands
        return kept

    def run_tail(operands):
        upstream, dnormed, kept = operands
        flat_up = upstream.astype(jnp.float32).reshape(-1, width)
        unused, pullback = jax.vjp(normalize, features.astype(jnp.float32), vectors)
        grad_field, grad_small = pullback(dnormed.reshape(features.shape))
        down_grad = (grad_field + flat_up.reshape(features.shape)).astype(jnp.bfloat16)
        return down_grad, grad_small

    def skip_tail(operands):
        upstream, dnormed, kept = operands
        return kept

    head = (
        jnp.zeros((pixels, width), jnp.bfloat16),
        jnp.zeros((pixels, hidden), jnp.bfloat16),
        jnp.zeros((pixels, width), jnp.float32),
        jnp.zeros((width,), jnp.float32),
        jnp.zeros((width,), jnp.float32),
        jnp.zeros((hidden,), jnp.float32),
    )
    tail = (jnp.zeros(feature_shape, jnp.bfloat16), jnp.zeros(vectors.shape, jnp.float32))
    held = leaving
    for tick_index in range(sections):
        active = section == sections - 1 - tick_index
        head = lax.cond(active, run_head, skip_head, (held, head))
        tail = lax.cond(active, run_tail, skip_tail, (held, head[2], tail))
        if tick_index + 1 < sections:
            held = from_behind(tail[0], "segment", -1)
    kept = tail[0]
    dproj_b, dpre_b, unused, grad_scale, grad_bias_out, grad_bias_in = head
    acc_second = lax.dot_general(
        activated, dproj_b, (((0,), (0,)), ((), ())), preferred_element_type=jnp.float32
    )
    acc_first = lax.dot_general(
        normed, dpre_b, (((0,), (0,)), ((), ())), preferred_element_type=jnp.float32
    )
    grad_small = tail[1]
    acc_small = jnp.concatenate(
        [
            grad_small[:52],
            grad_small[52:53] + grad_bias_out[None],
            grad_small[53:54] + grad_scale[None],
            grad_small[54:58] + grad_bias_in.reshape(4, width),
        ]
    )
    params_total = sections * (first_weight.size + second_weight.size + vectors.size)
    sum_first, sum_second, sum_small = sum_over((acc_first, acc_second, acc_small), "dp")
    own_sum = (
        jnp.sum(sum_first * sum_first)
        + jnp.sum(sum_second * sum_second)
        + jnp.sum(sum_small * sum_small)
    )
    squares = lax.psum(own_sum, "segment")
    factor = jnp.minimum(1.0, jnp.sqrt(jnp.float32(params_total)) * lax.rsqrt(squares + 1e-06))
    step_first = factor * sum_first
    step_second = factor * sum_second
    step_small = factor * sum_small
    input_grads = kept.reshape(batch_shape)
    return (input_grads[None], step_first[None], step_second[None], step_small[None])


def solution(mesh):
    in_specs = (
        P(None, "dp", None, None, None),
        P(None, "dp", None, None, None),
        P("segment", None, None),
        P("segment", None, None),
        P("segment", None, None),
    )
    out_specs = (
        P("segment", None, "dp", None, None, None),
        P("segment", None, None),
        P("segment", None, None),
        P("segment", None, None),
    )
    return jax.shard_map(
        per_device, mesh=mesh, in_specs=in_specs, out_specs=out_specs, check_vma=False
    )
```

```python
import jax
import jax.numpy as jnp
from jax import lax
from jax.sharding import PartitionSpec as P


def from_behind(value, axis, by):
    devices = lax.axis_size(axis)
    pairs = [(i, i + by) for i in range(devices) if 0 <= i + by < devices]
    return lax.ppermute(value, axis, pairs)


def halving_reduce(parts, axis, orders):
    count = lax.axis_size(axis)
    me = lax.axis_index(axis)
    current = list(parts)
    for step in range(len(orders[0])):
        sides = []
        sends = []
        for index, piece in enumerate(current):
            bit = orders[index][step]
            side = (me >> bit) & 1
            halves = piece.reshape((2, piece.shape[0] // 2) + piece.shape[1:])
            sends.append(lax.dynamic_index_in_dim(halves, 1 - side, 0, keepdims=False))
            sides.append((side, halves))
        got = [
            lax.ppermute(send, axis, [(j, j ^ (1 << orders[index][step])) for j in range(count)])
            for index, send in enumerate(sends)
        ]
        current = [
            lax.dynamic_index_in_dim(halves, side, 0, keepdims=False) + received
            for (side, halves), received in zip(sides, got)
        ]
    return current


def doubling_gather(parts, axis, orders):
    count = lax.axis_size(axis)
    me = lax.axis_index(axis)
    current = list(parts)
    for step in reversed(range(len(orders[0]))):
        got = [
            lax.ppermute(piece, axis, [(j, j ^ (1 << orders[index][step])) for j in range(count)])
            for index, piece in enumerate(current)
        ]
        joined = []
        for index, (piece, received) in enumerate(zip(current, got)):
            side = (me >> orders[index][step]) & 1
            both = jnp.zeros((2,) + piece.shape, piece.dtype)
            both = lax.dynamic_update_index_in_dim(both, piece, side, 0)
            both = lax.dynamic_update_index_in_dim(both, received, 1 - side, 0)
            joined.append(both.reshape((2 * piece.shape[0],) + piece.shape[1:]))
        current = joined
    return current


def sum_over(arrays, axis):
    count = lax.axis_size(axis)
    bits = count.bit_length() - 1
    if count != 1 << bits or bits < 2:
        return lax.psum(tuple(arrays), axis)
    first_grad, second_grad, small_grad = arrays
    rows = second_grad.shape[0] + small_grad.shape[0]
    unit = 8 * count
    total = -(-rows // unit) * unit
    joined = jnp.concatenate(
        [second_grad, small_grad, jnp.zeros((total - rows, small_grad.shape[1]), small_grad.dtype)]
    )
    orders = (list(range(bits)), [1, 0] + list(range(2, bits)))
    shards = halving_reduce([first_grad, joined], axis, orders)
    first_sum, joined_sum = doubling_gather(shards, axis, orders)
    second_rows = second_grad.shape[0]
    return (
        first_sum,
        joined_sum[:second_rows],
        joined_sum[second_rows : second_rows + small_grad.shape[0]],
    )


def depthwise(features, vectors):
    width = features.shape[-1]
    taps = vectors[:49].reshape(7, 7, 1, width)
    summed = lax.conv_general_dilated(
        features,
        taps,
        window_strides=(1, 1),
        padding=((3, 3), (3, 3)),
        dimension_numbers=("NHWC", "HWIO", "NHWC"),
        feature_group_count=width,
        precision=lax.Precision.HIGHEST,
    )
    return summed + vectors[49]


def normalize(features, vectors):
    conv = depthwise(features, vectors)
    average = jnp.mean(conv, axis=-1, keepdims=True)
    centered = conv - average
    variance = jnp.mean(centered * centered, axis=-1, keepdims=True)
    return centered * lax.rsqrt(variance + 1e-06) * vectors[50] + vectors[51]


def gelu_slope(preact):
    cumulative = 0.5 * (1.0 + jax.scipy.special.erf(preact * 0.7071067811865476))
    return cumulative + preact * jnp.exp(-0.5 * preact * preact) * 0.3989422804014327


def forward_block(features, first_weight, second_weight, vectors):
    width = features.shape[-1]
    normed = (
        normalize(features.astype(jnp.float32), vectors).astype(jnp.bfloat16).reshape(-1, width)
    )
    preact = jnp.dot(normed, first_weight, preferred_element_type=jnp.float32) + vectors[
        54:58
    ].reshape(-1)
    activated = jax.nn.gelu(preact, approximate=False).astype(jnp.bfloat16)
    projected = jnp.dot(activated, second_weight, preferred_element_type=jnp.float32) + vectors[52]
    output = (
        features.astype(jnp.float32) + vectors[53] * projected.reshape(features.shape)
    ).astype(jnp.bfloat16)
    return (output, normed, preact, activated, projected)


def backward_block(
    features, upstream, first_weight, second_weight, vectors, normed, preact, activated, projected
):
    width = features.shape[-1]
    flat_up = upstream.astype(jnp.float32).reshape(-1, width)
    grad_scale = jnp.sum(flat_up * projected, axis=0)
    dproj = flat_up * vectors[53]
    grad_bias_out = jnp.sum(dproj, axis=0)
    dproj_b = dproj.astype(jnp.bfloat16)
    grad_second = lax.dot_general(
        activated, dproj_b, (((0,), (0,)), ((), ())), preferred_element_type=jnp.float32
    )
    dact = lax.dot_general(
        dproj_b, second_weight, (((1,), (1,)), ((), ())), preferred_element_type=jnp.float32
    )
    dpre = dact * gelu_slope(preact)
    grad_bias_in = jnp.sum(dpre, axis=0)
    dpre_b = dpre.astype(jnp.bfloat16)
    grad_first = lax.dot_general(
        normed, dpre_b, (((0,), (0,)), ((), ())), preferred_element_type=jnp.float32
    )
    dnormed = lax.dot_general(
        dpre_b, first_weight, (((1,), (1,)), ((), ())), preferred_element_type=jnp.float32
    )
    unused, pullback = jax.vjp(normalize, features.astype(jnp.float32), vectors)
    grad_field, grad_small = pullback(dnormed.reshape(features.shape))
    grad_small = jnp.concatenate(
        [
            grad_small[:52],
            grad_small[52:53] + grad_bias_out[None],
            grad_small[53:54] + grad_scale[None],
            grad_small[54:58] + grad_bias_in.reshape(4, width),
        ]
    )
    down_grad = (grad_field + flat_up.reshape(features.shape)).astype(jnp.bfloat16)
    return (down_grad, grad_first, grad_second, grad_small)


def per_device(inputs, out_grad, w_in, w_out, vector_params):
    first_weight = w_in[0]
    second_weight = w_out[0]
    vectors = vector_params[0]
    section = lax.axis_index("segment")
    sections = lax.axis_size("segment")
    micro_count = inputs.shape[0]
    feature_shape = (micro_count * inputs.shape[1],) + inputs.shape[2:]
    batch_shape = inputs.shape
    width = feature_shape[-1]
    pixels = feature_shape[0] * feature_shape[1] * feature_shape[2]
    hidden = first_weight.shape[1]
    entering = inputs.reshape(feature_shape)
    leaving = out_grad.reshape(feature_shape)

    def run_forward(operands):
        features, stash = operands
        output, normed, preact, activated, projected = forward_block(
            features, first_weight, second_weight, vectors
        )
        return output, (features, normed, preact, activated, projected)

    def skip_forward(operands):
        features, stash = operands
        return jnp.zeros(feature_shape, jnp.bfloat16), stash

    stash = (
        jnp.zeros(feature_shape, jnp.bfloat16),
        jnp.zeros((pixels, width), jnp.bfloat16),
        jnp.zeros((pixels, hidden), jnp.float32),
        jnp.zeros((pixels, hidden), jnp.bfloat16),
        jnp.zeros((pixels, width), jnp.float32),
    )
    held = entering
    for tick_index in range(sections):
        output, stash = lax.cond(section == tick_index, run_forward, skip_forward, (held, stash))
        if tick_index + 1 < sections:
            held = from_behind(output, "segment", 1)

    features, normed, preact, activated, projected = stash

    def run_head(operands):
        upstream, kept = operands
        flat_up = upstream.astype(jnp.float32).reshape(-1, width)
        grad_scale = jnp.sum(flat_up * projected, axis=0)
        dproj = flat_up * vectors[53]
        grad_bias_out = jnp.sum(dproj, axis=0)
        dproj_b = dproj.astype(jnp.bfloat16)
        dact = lax.dot_general(
            dproj_b, second_weight, (((1,), (1,)), ((), ())), preferred_element_type=jnp.float32
        )
        dpre = dact * gelu_slope(preact)
        grad_bias_in = jnp.sum(dpre, axis=0)
        dpre_b = dpre.astype(jnp.bfloat16)
        dnormed = lax.dot_general(
            dpre_b, first_weight, (((1,), (1,)), ((), ())), preferred_element_type=jnp.float32
        )
        return (dproj_b, dpre_b, dnormed, grad_scale, grad_bias_out, grad_bias_in)

    def skip_head(operands):
        upstream, kept = operands
        return kept

    def run_tail(operands):
        upstream, dnormed, kept = operands
        flat_up = upstream.astype(jnp.float32).reshape(-1, width)
        unused, pullback = jax.vjp(normalize, features.astype(jnp.float32), vectors)
        grad_field, grad_small = pullback(dnormed.reshape(features.shape))
        down_grad = (grad_field + flat_up.reshape(features.shape)).astype(jnp.bfloat16)
        return down_grad, grad_small

    def skip_tail(operands):
        upstream, dnormed, kept = operands
        return kept

    head = (
        jnp.zeros((pixels, width), jnp.bfloat16),
        jnp.zeros((pixels, hidden), jnp.bfloat16),
        jnp.zeros((pixels, width), jnp.float32),
        jnp.zeros((width,), jnp.float32),
        jnp.zeros((width,), jnp.float32),
        jnp.zeros((hidden,), jnp.float32),
    )
    tail = (jnp.zeros(feature_shape, jnp.bfloat16), jnp.zeros(vectors.shape, jnp.float32))
    held = leaving
    for tick_index in range(sections):
        active = section == sections - 1 - tick_index
        head = lax.cond(active, run_head, skip_head, (held, head))
        tail = lax.cond(active, run_tail, skip_tail, (held, head[2], tail))
        if tick_index + 1 < sections:
            held = from_behind(tail[0], "segment", -1)
    kept = tail[0]
    dproj_b, dpre_b, unused, grad_scale, grad_bias_out, grad_bias_in = head
    acc_second = lax.dot_general(
        activated, dproj_b, (((0,), (0,)), ((), ())), preferred_element_type=jnp.float32
    )
    acc_first = lax.dot_general(
        normed, dpre_b, (((0,), (0,)), ((), ())), preferred_element_type=jnp.float32
    )
    grad_small = tail[1]
    acc_small = jnp.concatenate(
        [
            grad_small[:52],
            grad_small[52:53] + grad_bias_out[None],
            grad_small[53:54] + grad_scale[None],
            grad_small[54:58] + grad_bias_in.reshape(4, width),
        ]
    )
    params_total = sections * (first_weight.size + second_weight.size + vectors.size)
    sum_first, sum_second, sum_small = sum_over((acc_first, acc_second, acc_small), "dp")
    own_sum = (
        jnp.sum(sum_first * sum_first)
        + jnp.sum(sum_second * sum_second)
        + jnp.sum(sum_small * sum_small)
    )
    squares = lax.psum(own_sum, "segment")
    factor = jnp.minimum(1.0, jnp.sqrt(jnp.float32(params_total)) * lax.rsqrt(squares + 1e-06))
    step_first = factor * sum_first
    step_second = factor * sum_second
    step_small = factor * sum_small
    input_grads = kept.reshape(batch_shape)
    return (input_grads[None], step_first[None], step_second[None], step_small[None])


def solution(mesh):
    in_specs = (
        P(None, "dp", None, None, None),
        P(None, "dp", None, None, None),
        P("segment", None, None),
        P("segment", None, None),
        P("segment", None, None),
    )
    out_specs = (
        P("segment", None, "dp", None, None, None),
        P("segment", None, None),
        P("segment", None, None),
        P("segment", None, None),
    )
    return jax.shard_map(
        per_device, mesh=mesh, in_specs=in_specs, out_specs=out_specs, check_vma=False
    )
```

```python
import jax
import jax.numpy as jnp
from jax import lax
from jax.sharding import PartitionSpec as P


def from_behind(value, axis, by):
    devices = lax.axis_size(axis)
    pairs = [(i, i + by) for i in range(devices) if 0 <= i + by < devices]
    return lax.ppermute(value, axis, pairs)


def halving_reduce(parts, axis, orders):
    count = lax.axis_size(axis)
    me = lax.axis_index(axis)
    current = list(parts)
    for step in range(len(orders[0])):
        sides = []
        sends = []
        for index, piece in enumerate(current):
            bit = orders[index][step]
            side = (me >> bit) & 1
            halves = piece.reshape((2, piece.shape[0] // 2) + piece.shape[1:])
            sends.append(lax.dynamic_index_in_dim(halves, 1 - side, 0, keepdims=False))
            sides.append((side, halves))
        got = [
            lax.ppermute(send, axis, [(j, j ^ (1 << orders[index][step])) for j in range(count)])
            for index, send in enumerate(sends)
        ]
        current = [
            lax.dynamic_index_in_dim(halves, side, 0, keepdims=False) + received
            for (side, halves), received in zip(sides, got)
        ]
    return current


def doubling_gather(parts, axis, orders):
    count = lax.axis_size(axis)
    me = lax.axis_index(axis)
    current = list(parts)
    for step in reversed(range(len(orders[0]))):
        got = [
            lax.ppermute(piece, axis, [(j, j ^ (1 << orders[index][step])) for j in range(count)])
            for index, piece in enumerate(current)
        ]
        joined = []
        for index, (piece, received) in enumerate(zip(current, got)):
            side = (me >> orders[index][step]) & 1
            both = jnp.zeros((2,) + piece.shape, piece.dtype)
            both = lax.dynamic_update_index_in_dim(both, piece, side, 0)
            both = lax.dynamic_update_index_in_dim(both, received, 1 - side, 0)
            joined.append(both.reshape((2 * piece.shape[0],) + piece.shape[1:]))
        current = joined
    return current


def sum_over(arrays, axis):
    count = lax.axis_size(axis)
    bits = count.bit_length() - 1
    if count != 1 << bits or bits < 2:
        return lax.psum(tuple(arrays), axis)
    first_grad, second_grad, small_grad = arrays
    rows = second_grad.shape[0] + small_grad.shape[0]
    unit = 8 * count
    total = -(-rows // unit) * unit
    joined = jnp.concatenate(
        [second_grad, small_grad, jnp.zeros((total - rows, small_grad.shape[1]), small_grad.dtype)]
    )
    orders = (list(range(bits)), [1, 0] + list(range(2, bits)))
    shards = halving_reduce([first_grad, joined], axis, orders)
    first_sum, joined_sum = doubling_gather(shards, axis, orders)
    second_rows = second_grad.shape[0]
    return (
        first_sum,
        joined_sum[:second_rows],
        joined_sum[second_rows : second_rows + small_grad.shape[0]],
    )


def depthwise(features, vectors):
    height = features.shape[1]
    breadth = features.shape[2]
    padded = jnp.pad(features, ((0, 0), (3, 3), (3, 3), (0, 0)))
    summed = jnp.zeros(features.shape, jnp.float32)
    for row_shift in range(7):
        for col_shift in range(7):
            summed = (
                summed
                + padded[:, row_shift : row_shift + height, col_shift : col_shift + breadth, :]
                * vectors[row_shift * 7 + col_shift]
            )
    return summed + vectors[49]


def normalize(features, vectors):
    conv = depthwise(features, vectors)
    average = jnp.mean(conv, axis=-1, keepdims=True)
    centered = conv - average
    variance = jnp.mean(centered * centered, axis=-1, keepdims=True)
    return centered * lax.rsqrt(variance + 1e-06) * vectors[50] + vectors[51]


def gelu_slope(preact):
    cumulative = 0.5 * (1.0 + jax.scipy.special.erf(preact * 0.7071067811865476))
    return cumulative + preact * jnp.exp(-0.5 * preact * preact) * 0.3989422804014327


def forward_block(features, first_weight, second_weight, vectors):
    width = features.shape[-1]
    normed = (
        normalize(features.astype(jnp.float32), vectors).astype(jnp.bfloat16).reshape(-1, width)
    )
    preact = jnp.dot(normed, first_weight, preferred_element_type=jnp.float32) + vectors[
        54:58
    ].reshape(-1)
    activated = jax.nn.gelu(preact, approximate=False).astype(jnp.bfloat16)
    projected = jnp.dot(activated, second_weight, preferred_element_type=jnp.float32) + vectors[52]
    output = (
        features.astype(jnp.float32) + vectors[53] * projected.reshape(features.shape)
    ).astype(jnp.bfloat16)
    return (output, normed, preact, activated, projected)


def backward_block(
    features, upstream, first_weight, second_weight, vectors, normed, preact, activated, projected
):
    width = features.shape[-1]
    flat_up = upstream.astype(jnp.float32).reshape(-1, width)
    grad_scale = jnp.sum(flat_up * projected, axis=0)
    dproj = flat_up * vectors[53]
    grad_bias_out = jnp.sum(dproj, axis=0)
    dproj_b = dproj.astype(jnp.bfloat16)
    grad_second = lax.dot_general(
        activated, dproj_b, (((0,), (0,)), ((), ())), preferred_element_type=jnp.float32
    )
    dact = lax.dot_general(
        dproj_b, second_weight, (((1,), (1,)), ((), ())), preferred_element_type=jnp.float32
    )
    dpre = dact * gelu_slope(preact)
    grad_bias_in = jnp.sum(dpre, axis=0)
    dpre_b = dpre.astype(jnp.bfloat16)
    grad_first = lax.dot_general(
        normed, dpre_b, (((0,), (0,)), ((), ())), preferred_element_type=jnp.float32
    )
    dnormed = lax.dot_general(
        dpre_b, first_weight, (((1,), (1,)), ((), ())), preferred_element_type=jnp.float32
    )
    unused, pullback = jax.vjp(normalize, features.astype(jnp.float32), vectors)
    grad_field, grad_small = pullback(dnormed.reshape(features.shape))
    grad_small = jnp.concatenate(
        [
            grad_small[:52],
            grad_small[52:53] + grad_bias_out[None],
            grad_small[53:54] + grad_scale[None],
            grad_small[54:58] + grad_bias_in.reshape(4, width),
        ]
    )
    down_grad = (grad_field + flat_up.reshape(features.shape)).astype(jnp.bfloat16)
    return (down_grad, grad_first, grad_second, grad_small)


def per_device(inputs, out_grad, w_in, w_out, vector_params):
    first_weight = w_in[0]
    second_weight = w_out[0]
    vectors = vector_params[0]
    section = lax.axis_index("segment")
    sections = lax.axis_size("segment")
    micro_count = inputs.shape[0]
    feature_shape = (micro_count * inputs.shape[1],) + inputs.shape[2:]
    batch_shape = inputs.shape
    width = feature_shape[-1]
    pixels = feature_shape[0] * feature_shape[1] * feature_shape[2]
    hidden = first_weight.shape[1]
    entering = inputs.reshape(feature_shape)
    leaving = out_grad.reshape(feature_shape)

    def run_forward(operands):
        features, stash = operands
        output, normed, preact, activated, projected = forward_block(
            features, first_weight, second_weight, vectors
        )
        return output, (features, normed, preact, activated, projected)

    def skip_forward(operands):
        features, stash = operands
        return jnp.zeros(feature_shape, jnp.bfloat16), stash

    stash = (
        jnp.zeros(feature_shape, jnp.bfloat16),
        jnp.zeros((pixels, width), jnp.bfloat16),
        jnp.zeros((pixels, hidden), jnp.float32),
        jnp.zeros((pixels, hidden), jnp.bfloat16),
        jnp.zeros((pixels, width), jnp.float32),
    )
    held = entering
    for tick_index in range(sections):
        output, stash = lax.cond(section == tick_index, run_forward, skip_forward, (held, stash))
        if tick_index + 1 < sections:
            held = from_behind(output, "segment", 1)

    features, normed, preact, activated, projected = stash

    def run_head(operands):
        upstream, kept = operands
        flat_up = upstream.astype(jnp.float32).reshape(-1, width)
        grad_scale = jnp.sum(flat_up * projected, axis=0)
        dproj = flat_up * vectors[53]
        grad_bias_out = jnp.sum(dproj, axis=0)
        dproj_b = dproj.astype(jnp.bfloat16)
        dact = lax.dot_general(
            dproj_b, second_weight, (((1,), (1,)), ((), ())), preferred_element_type=jnp.float32
        )
        dpre = dact * gelu_slope(preact)
        grad_bias_in = jnp.sum(dpre, axis=0)
        dpre_b = dpre.astype(jnp.bfloat16)
        dnormed = lax.dot_general(
            dpre_b, first_weight, (((1,), (1,)), ((), ())), preferred_element_type=jnp.float32
        )
        return (dproj_b, dpre_b, dnormed, grad_scale, grad_bias_out, grad_bias_in)

    def skip_head(operands):
        upstream, kept = operands
        return kept

    def run_tail(operands):
        upstream, dnormed, kept = operands
        flat_up = upstream.astype(jnp.float32).reshape(-1, width)
        unused, pullback = jax.vjp(
            lambda field: normalize(field, vectors), features.astype(jnp.float32)
        )
        (grad_field,) = pullback(dnormed.reshape(features.shape))
        down_grad = (grad_field + flat_up.reshape(features.shape)).astype(jnp.bfloat16)
        return down_grad

    def skip_tail(operands):
        upstream, dnormed, kept = operands
        return kept

    head = (
        jnp.zeros((pixels, width), jnp.bfloat16),
        jnp.zeros((pixels, hidden), jnp.bfloat16),
        jnp.zeros((pixels, width), jnp.float32),
        jnp.zeros((width,), jnp.float32),
        jnp.zeros((width,), jnp.float32),
        jnp.zeros((hidden,), jnp.float32),
    )
    tail = jnp.zeros(feature_shape, jnp.bfloat16)
    held = leaving
    for tick_index in range(sections):
        active = section == sections - 1 - tick_index
        head = lax.cond(active, run_head, skip_head, (held, head))
        tail = lax.cond(active, run_tail, skip_tail, (held, head[2], tail))
        if tick_index + 1 < sections:
            held = from_behind(tail, "segment", -1)
    kept = tail
    dproj_b, dpre_b, dnormed, grad_scale, grad_bias_out, grad_bias_in = head
    acc_second = lax.dot_general(
        activated, dproj_b, (((0,), (0,)), ((), ())), preferred_element_type=jnp.float32
    )
    acc_first = lax.dot_general(
        normed, dpre_b, (((0,), (0,)), ((), ())), preferred_element_type=jnp.float32
    )
    unused, pullback = jax.vjp(
        lambda small: normalize(features.astype(jnp.float32), small), vectors
    )
    (grad_small,) = pullback(dnormed.reshape(features.shape))
    acc_small = jnp.concatenate(
        [
            grad_small[:52],
            grad_small[52:53] + grad_bias_out[None],
            grad_small[53:54] + grad_scale[None],
            grad_small[54:58] + grad_bias_in.reshape(4, width),
        ]
    )
    params_total = sections * (first_weight.size + second_weight.size + vectors.size)
    sum_first, sum_second, sum_small = sum_over((acc_first, acc_second, acc_small), "dp")
    own_sum = (
        jnp.sum(sum_first * sum_first)
        + jnp.sum(sum_second * sum_second)
        + jnp.sum(sum_small * sum_small)
    )
    squares = lax.psum(own_sum, "segment")
    factor = jnp.minimum(1.0, jnp.sqrt(jnp.float32(params_total)) * lax.rsqrt(squares + 1e-06))
    step_first = factor * sum_first
    step_second = factor * sum_second
    step_small = factor * sum_small
    input_grads = kept.reshape(batch_shape)
    return (input_grads[None], step_first[None], step_second[None], step_small[None])


def solution(mesh):
    in_specs = (
        P(None, "dp", None, None, None),
        P(None, "dp", None, None, None),
        P("segment", None, None),
        P("segment", None, None),
        P("segment", None, None),
    )
    out_specs = (
        P("segment", None, "dp", None, None, None),
        P("segment", None, None),
        P("segment", None, None),
        P("segment", None, None),
    )
    return jax.shard_map(
        per_device, mesh=mesh, in_specs=in_specs, out_specs=out_specs, check_vma=False
    )
```

```python
import jax
import jax.numpy as jnp
from jax import lax
from jax.sharding import PartitionSpec as P


def from_behind(value, axis, by):
    devices = lax.axis_size(axis)
    pairs = [(i, i + by) for i in range(devices) if 0 <= i + by < devices]
    return lax.ppermute(value, axis, pairs)


def halving_reduce(parts, axis, orders):
    count = lax.axis_size(axis)
    me = lax.axis_index(axis)
    current = list(parts)
    for step in range(len(orders[0])):
        sides = []
        sends = []
        for index, piece in enumerate(current):
            bit = orders[index][step]
            side = (me >> bit) & 1
            halves = piece.reshape((2, piece.shape[0] // 2) + piece.shape[1:])
            sends.append(lax.dynamic_index_in_dim(halves, 1 - side, 0, keepdims=False))
            sides.append((side, halves))
        got = [
            lax.ppermute(send, axis, [(j, j ^ (1 << orders[index][step])) for j in range(count)])
            for index, send in enumerate(sends)
        ]
        current = [
            lax.dynamic_index_in_dim(halves, side, 0, keepdims=False) + received
            for (side, halves), received in zip(sides, got)
        ]
    return current


def doubling_gather(parts, axis, orders):
    count = lax.axis_size(axis)
    me = lax.axis_index(axis)
    current = list(parts)
    for step in reversed(range(len(orders[0]))):
        got = [
            lax.ppermute(piece, axis, [(j, j ^ (1 << orders[index][step])) for j in range(count)])
            for index, piece in enumerate(current)
        ]
        joined = []
        for index, (piece, received) in enumerate(zip(current, got)):
            side = (me >> orders[index][step]) & 1
            both = jnp.zeros((2,) + piece.shape, piece.dtype)
            both = lax.dynamic_update_index_in_dim(both, piece, side, 0)
            both = lax.dynamic_update_index_in_dim(both, received, 1 - side, 0)
            joined.append(both.reshape((2 * piece.shape[0],) + piece.shape[1:]))
        current = joined
    return current


def sum_over(arrays, axis):
    count = lax.axis_size(axis)
    bits = count.bit_length() - 1
    if count != 1 << bits or bits < 2:
        return lax.psum(tuple(arrays), axis)
    first_grad, second_grad, small_grad = arrays
    rows = second_grad.shape[0] + small_grad.shape[0]
    unit = 8 * count
    total = -(-rows // unit) * unit
    joined = jnp.concatenate(
        [second_grad, small_grad, jnp.zeros((total - rows, small_grad.shape[1]), small_grad.dtype)]
    )
    orders = (list(range(bits)), [1, 0] + list(range(2, bits)))
    shards = halving_reduce([first_grad, joined], axis, orders)
    first_sum, joined_sum = doubling_gather(shards, axis, orders)
    second_rows = second_grad.shape[0]
    return (
        first_sum,
        joined_sum[:second_rows],
        joined_sum[second_rows : second_rows + small_grad.shape[0]],
    )


def depthwise(features, vectors):
    height = features.shape[1]
    breadth = features.shape[2]
    padded = jnp.pad(features, ((0, 0), (3, 3), (3, 3), (0, 0)))
    summed = jnp.zeros(features.shape, jnp.float32)
    for row_shift in range(7):
        for col_shift in range(7):
            summed = (
                summed
                + padded[:, row_shift : row_shift + height, col_shift : col_shift + breadth, :]
                * vectors[row_shift * 7 + col_shift]
            )
    return summed + vectors[49]


def normalize(features, vectors):
    conv = depthwise(features, vectors)
    average = jnp.mean(conv, axis=-1, keepdims=True)
    centered = conv - average
    variance = jnp.mean(centered * centered, axis=-1, keepdims=True)
    return centered * lax.rsqrt(variance + 1e-06) * vectors[50] + vectors[51]


def gelu_slope(preact):
    cumulative = 0.5 * (1.0 + jax.scipy.special.erf(preact * 0.7071067811865476))
    return cumulative + preact * jnp.exp(-0.5 * preact * preact) * 0.3989422804014327


def forward_block(features, first_weight, second_weight, vectors):
    width = features.shape[-1]
    normed = (
        normalize(features.astype(jnp.float32), vectors).astype(jnp.bfloat16).reshape(-1, width)
    )
    preact = jnp.dot(normed, first_weight, preferred_element_type=jnp.float32) + vectors[
        54:58
    ].reshape(-1)
    activated = jax.nn.gelu(preact, approximate=False).astype(jnp.bfloat16)
    projected = jnp.dot(activated, second_weight, preferred_element_type=jnp.float32) + vectors[52]
    output = (
        features.astype(jnp.float32) + vectors[53] * projected.reshape(features.shape)
    ).astype(jnp.bfloat16)
    return (output, normed, preact, activated, projected)


def backward_block(
    features, upstream, first_weight, second_weight, vectors, normed, preact, activated, projected
):
    width = features.shape[-1]
    flat_up = upstream.astype(jnp.float32).reshape(-1, width)
    grad_scale = jnp.sum(flat_up * projected, axis=0)
    dproj = flat_up * vectors[53]
    grad_bias_out = jnp.sum(dproj, axis=0)
    dproj_b = dproj.astype(jnp.bfloat16)
    grad_second = lax.dot_general(
        activated, dproj_b, (((0,), (0,)), ((), ())), preferred_element_type=jnp.float32
    )
    dact = lax.dot_general(
        dproj_b, second_weight, (((1,), (1,)), ((), ())), preferred_element_type=jnp.float32
    )
    dpre = dact * gelu_slope(preact)
    grad_bias_in = jnp.sum(dpre, axis=0)
    dpre_b = dpre.astype(jnp.bfloat16)
    grad_first = lax.dot_general(
        normed, dpre_b, (((0,), (0,)), ((), ())), preferred_element_type=jnp.float32
    )
    dnormed = lax.dot_general(
        dpre_b, first_weight, (((1,), (1,)), ((), ())), preferred_element_type=jnp.float32
    )
    unused, pullback = jax.vjp(normalize, features.astype(jnp.float32), vectors)
    grad_field, grad_small = pullback(dnormed.reshape(features.shape))
    grad_small = jnp.concatenate(
        [
            grad_small[:52],
            grad_small[52:53] + grad_bias_out[None],
            grad_small[53:54] + grad_scale[None],
            grad_small[54:58] + grad_bias_in.reshape(4, width),
        ]
    )
    down_grad = (grad_field + flat_up.reshape(features.shape)).astype(jnp.bfloat16)
    return (down_grad, grad_first, grad_second, grad_small)


def per_device(inputs, out_grad, w_in, w_out, vector_params):
    first_weight = w_in[0]
    second_weight = w_out[0]
    vectors = vector_params[0]
    section = lax.axis_index("segment")
    sections = lax.axis_size("segment")
    micro_count = inputs.shape[0]
    feature_shape = (micro_count * inputs.shape[1],) + inputs.shape[2:]
    batch_shape = inputs.shape
    width = feature_shape[-1]
    pixels = feature_shape[0] * feature_shape[1] * feature_shape[2]
    hidden = first_weight.shape[1]
    entering = inputs.reshape(feature_shape)
    leaving = out_grad.reshape(feature_shape)

    def run_forward(operands):
        features, stash = operands
        output, normed, preact, activated, projected = forward_block(
            features, first_weight, second_weight, vectors
        )
        return output, (features, normed, preact, activated, projected)

    def skip_forward(operands):
        features, stash = operands
        return jnp.zeros(feature_shape, jnp.bfloat16), stash

    stash = (
        jnp.zeros(feature_shape, jnp.bfloat16),
        jnp.zeros((pixels, width), jnp.bfloat16),
        jnp.zeros((pixels, hidden), jnp.float32),
        jnp.zeros((pixels, hidden), jnp.bfloat16),
        jnp.zeros((pixels, width), jnp.float32),
    )
    def forward_tick(tick_index, carry):
        held, stash = carry
        output, stash = lax.cond(section == tick_index, run_forward, skip_forward, (held, stash))
        return from_behind(output, "segment", 1), stash

    held, stash = lax.fori_loop(0, sections - 1, forward_tick, (entering, stash))
    output, stash = lax.cond(section == sections - 1, run_forward, skip_forward, (held, stash))

    features, normed, preact, activated, projected = stash

    def run_head(operands):
        upstream, kept = operands
        flat_up = upstream.astype(jnp.float32).reshape(-1, width)
        grad_scale = jnp.sum(flat_up * projected, axis=0)
        dproj = flat_up * vectors[53]
        grad_bias_out = jnp.sum(dproj, axis=0)
        dproj_b = dproj.astype(jnp.bfloat16)
        dact = lax.dot_general(
            dproj_b, second_weight, (((1,), (1,)), ((), ())), preferred_element_type=jnp.float32
        )
        dpre = dact * gelu_slope(preact)
        grad_bias_in = jnp.sum(dpre, axis=0)
        dpre_b = dpre.astype(jnp.bfloat16)
        dnormed = lax.dot_general(
            dpre_b, first_weight, (((1,), (1,)), ((), ())), preferred_element_type=jnp.float32
        )
        return (dproj_b, dpre_b, dnormed, grad_scale, grad_bias_out, grad_bias_in)

    def skip_head(operands):
        upstream, kept = operands
        return kept

    def run_tail(operands):
        upstream, dnormed, kept = operands
        flat_up = upstream.astype(jnp.float32).reshape(-1, width)
        unused, pullback = jax.vjp(normalize, features.astype(jnp.float32), vectors)
        grad_field, grad_small = pullback(dnormed.reshape(features.shape))
        down_grad = (grad_field + flat_up.reshape(features.shape)).astype(jnp.bfloat16)
        return down_grad, grad_small

    def skip_tail(operands):
        upstream, dnormed, kept = operands
        return kept

    head = (
        jnp.zeros((pixels, width), jnp.bfloat16),
        jnp.zeros((pixels, hidden), jnp.bfloat16),
        jnp.zeros((pixels, width), jnp.float32),
        jnp.zeros((width,), jnp.float32),
        jnp.zeros((width,), jnp.float32),
        jnp.zeros((hidden,), jnp.float32),
    )
    tail = (jnp.zeros(feature_shape, jnp.bfloat16), jnp.zeros(vectors.shape, jnp.float32))
    def backward_tick(tick_index, carry):
        held, head, tail = carry
        active = section == sections - 1 - tick_index
        head = lax.cond(active, run_head, skip_head, (held, head))
        tail = lax.cond(active, run_tail, skip_tail, (held, head[2], tail))
        return from_behind(tail[0], "segment", -1), head, tail

    held, head, tail = lax.fori_loop(0, sections - 1, backward_tick, (leaving, head, tail))
    head = lax.cond(section == 0, run_head, skip_head, (held, head))
    tail = lax.cond(section == 0, run_tail, skip_tail, (held, head[2], tail))
    kept = tail[0]
    dproj_b, dpre_b, unused, grad_scale, grad_bias_out, grad_bias_in = head
    acc_second = lax.dot_general(
        activated, dproj_b, (((0,), (0,)), ((), ())), preferred_element_type=jnp.float32
    )
    acc_first = lax.dot_general(
        normed, dpre_b, (((0,), (0,)), ((), ())), preferred_element_type=jnp.float32
    )
    grad_small = tail[1]
    acc_small = jnp.concatenate(
        [
            grad_small[:52],
            grad_small[52:53] + grad_bias_out[None],
            grad_small[53:54] + grad_scale[None],
            grad_small[54:58] + grad_bias_in.reshape(4, width),
        ]
    )
    params_total = sections * (first_weight.size + second_weight.size + vectors.size)
    sum_first, sum_second, sum_small = sum_over((acc_first, acc_second, acc_small), "dp")
    own_sum = (
        jnp.sum(sum_first * sum_first)
        + jnp.sum(sum_second * sum_second)
        + jnp.sum(sum_small * sum_small)
    )
    squares = lax.psum(own_sum, "segment")
    factor = jnp.minimum(1.0, jnp.sqrt(jnp.float32(params_total)) * lax.rsqrt(squares + 1e-06))
    step_first = factor * sum_first
    step_second = factor * sum_second
    step_small = factor * sum_small
    input_grads = kept.reshape(batch_shape)
    return (input_grads[None], step_first[None], step_second[None], step_small[None])


def solution(mesh):
    in_specs = (
        P(None, "dp", None, None, None),
        P(None, "dp", None, None, None),
        P("segment", None, None),
        P("segment", None, None),
        P("segment", None, None),
    )
    out_specs = (
        P("segment", None, "dp", None, None, None),
        P("segment", None, None),
        P("segment", None, None),
        P("segment", None, None),
    )
    return jax.shard_map(
        per_device, mesh=mesh, in_specs=in_specs, out_specs=out_specs, check_vma=False
    )
```

```python
import jax
import jax.numpy as jnp
from jax import lax
from jax.sharding import PartitionSpec as P


def from_behind(value, axis, by):
    devices = lax.axis_size(axis)
    pairs = [(i, i + by) for i in range(devices) if 0 <= i + by < devices]
    return lax.ppermute(value, axis, pairs)


def halving_reduce(parts, axis, orders):
    count = lax.axis_size(axis)
    me = lax.axis_index(axis)
    current = list(parts)
    for step in range(len(orders[0])):
        sides = []
        sends = []
        for index, piece in enumerate(current):
            bit = orders[index][step]
            side = (me >> bit) & 1
            halves = piece.reshape((2, piece.shape[0] // 2) + piece.shape[1:])
            sends.append(lax.dynamic_index_in_dim(halves, 1 - side, 0, keepdims=False))
            sides.append((side, halves))
        got = [
            lax.ppermute(send, axis, [(j, j ^ (1 << orders[index][step])) for j in range(count)])
            for index, send in enumerate(sends)
        ]
        current = [
            lax.dynamic_index_in_dim(halves, side, 0, keepdims=False) + received
            for (side, halves), received in zip(sides, got)
        ]
    return current


def doubling_gather(parts, axis, orders):
    count = lax.axis_size(axis)
    me = lax.axis_index(axis)
    current = list(parts)
    for step in reversed(range(len(orders[0]))):
        got = [
            lax.ppermute(piece, axis, [(j, j ^ (1 << orders[index][step])) for j in range(count)])
            for index, piece in enumerate(current)
        ]
        joined = []
        for index, (piece, received) in enumerate(zip(current, got)):
            side = (me >> orders[index][step]) & 1
            both = jnp.zeros((2,) + piece.shape, piece.dtype)
            both = lax.dynamic_update_index_in_dim(both, piece, side, 0)
            both = lax.dynamic_update_index_in_dim(both, received, 1 - side, 0)
            joined.append(both.reshape((2 * piece.shape[0],) + piece.shape[1:]))
        current = joined
    return current


def sum_over(arrays, axis):
    count = lax.axis_size(axis)
    bits = count.bit_length() - 1
    if count != 1 << bits or bits < 2:
        return lax.psum(tuple(arrays), axis)
    first_grad, second_grad, small_grad = arrays
    rows = second_grad.shape[0] + small_grad.shape[0]
    unit = 8 * count
    total = -(-rows // unit) * unit
    joined = jnp.concatenate(
        [second_grad, small_grad, jnp.zeros((total - rows, small_grad.shape[1]), small_grad.dtype)]
    )
    orders = (list(range(bits)), [1, 0] + list(range(2, bits)))
    shards = halving_reduce([first_grad, joined], axis, orders)
    first_sum, joined_sum = doubling_gather(shards, axis, orders)
    second_rows = second_grad.shape[0]
    return (
        first_sum,
        joined_sum[:second_rows],
        joined_sum[second_rows : second_rows + small_grad.shape[0]],
    )


def depthwise(features, vectors):
    height = features.shape[1]
    breadth = features.shape[2]
    padded = jnp.pad(features, ((0, 0), (3, 3), (3, 3), (0, 0)))
    summed = jnp.zeros(features.shape, jnp.float32)
    for row_shift in range(7):
        for col_shift in range(7):
            summed = (
                summed
                + padded[:, row_shift : row_shift + height, col_shift : col_shift + breadth, :]
                * vectors[row_shift * 7 + col_shift]
            )
    return summed + vectors[49]


def normalize(features, vectors):
    conv = depthwise(features, vectors)
    average = jnp.mean(conv, axis=-1, keepdims=True)
    centered = conv - average
    variance = jnp.mean(centered * centered, axis=-1, keepdims=True)
    return centered * lax.rsqrt(variance + 1e-06) * vectors[50] + vectors[51]


def gelu_slope(preact):
    cumulative = 0.5 * (1.0 + jax.scipy.special.erf(preact * 0.7071067811865476))
    return cumulative + preact * jnp.exp(-0.5 * preact * preact) * 0.3989422804014327


def forward_block(features, first_weight, second_weight, vectors):
    width = features.shape[-1]
    normed = (
        normalize(features.astype(jnp.float32), vectors).astype(jnp.bfloat16).reshape(-1, width)
    )
    preact = jnp.dot(normed, first_weight, preferred_element_type=jnp.float32) + vectors[
        54:58
    ].reshape(-1)
    activated = jax.nn.gelu(preact, approximate=False).astype(jnp.bfloat16)
    projected = jnp.dot(activated, second_weight, preferred_element_type=jnp.float32) + vectors[52]
    output = (
        features.astype(jnp.float32) + vectors[53] * projected.reshape(features.shape)
    ).astype(jnp.bfloat16)
    return (output, normed, preact, activated, projected)


def backward_block(
    features, upstream, first_weight, second_weight, vectors, normed, preact, activated, projected
):
    width = features.shape[-1]
    flat_up = upstream.astype(jnp.float32).reshape(-1, width)
    grad_scale = jnp.sum(flat_up * projected, axis=0)
    dproj = flat_up * vectors[53]
    grad_bias_out = jnp.sum(dproj, axis=0)
    dproj_b = dproj.astype(jnp.bfloat16)
    grad_second = lax.dot_general(
        activated, dproj_b, (((0,), (0,)), ((), ())), preferred_element_type=jnp.float32
    )
    dact = lax.dot_general(
        dproj_b, second_weight, (((1,), (1,)), ((), ())), preferred_element_type=jnp.float32
    )
    dpre = dact * gelu_slope(preact)
    grad_bias_in = jnp.sum(dpre, axis=0)
    dpre_b = dpre.astype(jnp.bfloat16)
    grad_first = lax.dot_general(
        normed, dpre_b, (((0,), (0,)), ((), ())), preferred_element_type=jnp.float32
    )
    dnormed = lax.dot_general(
        dpre_b, first_weight, (((1,), (1,)), ((), ())), preferred_element_type=jnp.float32
    )
    unused, pullback = jax.vjp(normalize, features.astype(jnp.float32), vectors)
    grad_field, grad_small = pullback(dnormed.reshape(features.shape))
    grad_small = jnp.concatenate(
        [
            grad_small[:52],
            grad_small[52:53] + grad_bias_out[None],
            grad_small[53:54] + grad_scale[None],
            grad_small[54:58] + grad_bias_in.reshape(4, width),
        ]
    )
    down_grad = (grad_field + flat_up.reshape(features.shape)).astype(jnp.bfloat16)
    return (down_grad, grad_first, grad_second, grad_small)


def per_device(inputs, out_grad, w_in, w_out, vector_params):
    first_weight = w_in[0]
    second_weight = w_out[0]
    vectors = vector_params[0]
    section = lax.axis_index("segment")
    sections = lax.axis_size("segment")
    micro_count = inputs.shape[0]
    feature_shape = (micro_count * inputs.shape[1],) + inputs.shape[2:]
    batch_shape = inputs.shape
    width = feature_shape[-1]
    pixels = feature_shape[0] * feature_shape[1] * feature_shape[2]
    hidden = first_weight.shape[1]
    entering = inputs.reshape(feature_shape)
    leaving = out_grad.reshape(feature_shape)

    def run_forward(operands):
        features, stash = operands
        output, normed, preact, activated, projected = forward_block(
            features, first_weight, second_weight, vectors
        )
        return output, (features, normed, preact, activated, projected)

    def skip_forward(operands):
        features, stash = operands
        return jnp.zeros(feature_shape, jnp.bfloat16), stash

    stash = (
        jnp.zeros(feature_shape, jnp.bfloat16),
        jnp.zeros((pixels, width), jnp.bfloat16),
        jnp.zeros((pixels, hidden), jnp.float32),
        jnp.zeros((pixels, hidden), jnp.bfloat16),
        jnp.zeros((pixels, width), jnp.float32),
    )
    held = entering
    for tick_index in range(sections):
        output, stash = lax.cond(section == tick_index, run_forward, skip_forward, (held, stash))
        if tick_index + 1 < sections:
            held = from_behind(output, "segment", 1)

    features, normed, preact, activated, projected = stash

    def run_head(operands):
        upstream, kept = operands
        flat_up = upstream.astype(jnp.float32).reshape(-1, width)
        grad_scale = jnp.sum(flat_up * projected, axis=0)
        dproj = flat_up * vectors[53]
        grad_bias_out = jnp.sum(dproj, axis=0)
        dproj_b = dproj.astype(jnp.bfloat16)
        dact = lax.dot_general(
            dproj_b, second_weight, (((1,), (1,)), ((), ())), preferred_element_type=jnp.float32
        )
        dpre = dact * gelu_slope(preact)
        grad_bias_in = jnp.sum(dpre, axis=0)
        dpre_b = dpre.astype(jnp.bfloat16)
        dnormed = lax.dot_general(
            dpre_b, first_weight, (((1,), (1,)), ((), ())), preferred_element_type=jnp.float32
        )
        return (dproj_b, dpre_b, dnormed, grad_scale, grad_bias_out, grad_bias_in)

    def skip_head(operands):
        upstream, kept = operands
        return kept

    def run_tail(operands):
        upstream, dnormed, kept = operands
        flat_up = upstream.astype(jnp.float32).reshape(-1, width)
        unused, pullback = jax.vjp(normalize, features.astype(jnp.float32), vectors)
        grad_field, grad_small = pullback(dnormed.reshape(features.shape))
        down_grad = (grad_field + flat_up.reshape(features.shape)).astype(jnp.bfloat16)
        return down_grad, grad_small

    def skip_tail(operands):
        upstream, dnormed, kept = operands
        return kept

    def run_both(operands):
        upstream, head, tail = operands
        head = run_head((upstream, head))
        return head, run_tail((upstream, head[2], tail))

    def skip_both(operands):
        upstream, head, tail = operands
        return head, tail

    head = (
        jnp.zeros((pixels, width), jnp.bfloat16),
        jnp.zeros((pixels, hidden), jnp.bfloat16),
        jnp.zeros((pixels, width), jnp.float32),
        jnp.zeros((width,), jnp.float32),
        jnp.zeros((width,), jnp.float32),
        jnp.zeros((hidden,), jnp.float32),
    )
    tail = (jnp.zeros(feature_shape, jnp.bfloat16), jnp.zeros(vectors.shape, jnp.float32))
    held = leaving
    for tick_index in range(sections):
        active = section == sections - 1 - tick_index
        head, tail = lax.cond(active, run_both, skip_both, (held, head, tail))
        if tick_index + 1 < sections:
            held = from_behind(tail[0], "segment", -1)
    kept = tail[0]
    dproj_b, dpre_b, unused, grad_scale, grad_bias_out, grad_bias_in = head
    acc_second = lax.dot_general(
        activated, dproj_b, (((0,), (0,)), ((), ())), preferred_element_type=jnp.float32
    )
    acc_first = lax.dot_general(
        normed, dpre_b, (((0,), (0,)), ((), ())), preferred_element_type=jnp.float32
    )
    grad_small = tail[1]
    acc_small = jnp.concatenate(
        [
            grad_small[:52],
            grad_small[52:53] + grad_bias_out[None],
            grad_small[53:54] + grad_scale[None],
            grad_small[54:58] + grad_bias_in.reshape(4, width),
        ]
    )
    params_total = sections * (first_weight.size + second_weight.size + vectors.size)
    sum_first, sum_second, sum_small = sum_over((acc_first, acc_second, acc_small), "dp")
    own_sum = (
        jnp.sum(sum_first * sum_first)
        + jnp.sum(sum_second * sum_second)
        + jnp.sum(sum_small * sum_small)
    )
    squares = lax.psum(own_sum, "segment")
    factor = jnp.minimum(1.0, jnp.sqrt(jnp.float32(params_total)) * lax.rsqrt(squares + 1e-06))
    step_first = factor * sum_first
    step_second = factor * sum_second
    step_small = factor * sum_small
    input_grads = kept.reshape(batch_shape)
    return (input_grads[None], step_first[None], step_second[None], step_small[None])


def solution(mesh):
    in_specs = (
        P(None, "dp", None, None, None),
        P(None, "dp", None, None, None),
        P("segment", None, None),
        P("segment", None, None),
        P("segment", None, None),
    )
    out_specs = (
        P("segment", None, "dp", None, None, None),
        P("segment", None, None),
        P("segment", None, None),
        P("segment", None, None),
    )
    return jax.shard_map(
        per_device, mesh=mesh, in_specs=in_specs, out_specs=out_specs, check_vma=False
    )
```

```python
import jax
import jax.numpy as jnp
from jax import lax
from jax.sharding import PartitionSpec as P


def from_behind(value, axis, by):
    devices = lax.axis_size(axis)
    pairs = [(i, i + by) for i in range(devices) if 0 <= i + by < devices]
    return lax.ppermute(value, axis, pairs)


def halving_reduce(parts, axis, orders):
    count = lax.axis_size(axis)
    me = lax.axis_index(axis)
    current = list(parts)
    for step in range(len(orders[0])):
        sides = []
        sends = []
        for index, piece in enumerate(current):
            bit = orders[index][step]
            side = (me >> bit) & 1
            halves = piece.reshape((2, piece.shape[0] // 2) + piece.shape[1:])
            sends.append(lax.dynamic_index_in_dim(halves, 1 - side, 0, keepdims=False))
            sides.append((side, halves))
        got = [
            lax.ppermute(send, axis, [(j, j ^ (1 << orders[index][step])) for j in range(count)])
            for index, send in enumerate(sends)
        ]
        current = [
            lax.dynamic_index_in_dim(halves, side, 0, keepdims=False) + received
            for (side, halves), received in zip(sides, got)
        ]
    return current


def doubling_gather(parts, axis, orders):
    count = lax.axis_size(axis)
    me = lax.axis_index(axis)
    current = list(parts)
    for step in reversed(range(len(orders[0]))):
        got = [
            lax.ppermute(piece, axis, [(j, j ^ (1 << orders[index][step])) for j in range(count)])
            for index, piece in enumerate(current)
        ]
        joined = []
        for index, (piece, received) in enumerate(zip(current, got)):
            side = (me >> orders[index][step]) & 1
            both = jnp.zeros((2,) + piece.shape, piece.dtype)
            both = lax.dynamic_update_index_in_dim(both, piece, side, 0)
            both = lax.dynamic_update_index_in_dim(both, received, 1 - side, 0)
            joined.append(both.reshape((2 * piece.shape[0],) + piece.shape[1:]))
        current = joined
    return current


def sum_over(arrays, axis):
    count = lax.axis_size(axis)
    bits = count.bit_length() - 1
    if count != 1 << bits or bits < 2:
        return lax.psum(tuple(arrays), axis)
    first_grad, second_grad, small_grad = arrays
    rows = second_grad.shape[0] + small_grad.shape[0]
    unit = 8 * count
    total = -(-rows // unit) * unit
    joined = jnp.concatenate(
        [second_grad, small_grad, jnp.zeros((total - rows, small_grad.shape[1]), small_grad.dtype)]
    )
    orders = (list(range(bits)), [1, 0] + list(range(2, bits)))
    shards = halving_reduce([first_grad, joined], axis, orders)
    first_sum, joined_sum = doubling_gather(shards, axis, orders)
    second_rows = second_grad.shape[0]
    return (
        first_sum,
        joined_sum[:second_rows],
        joined_sum[second_rows : second_rows + small_grad.shape[0]],
    )


def depthwise(features, vectors):
    height = features.shape[1]
    breadth = features.shape[2]
    padded = jnp.pad(features, ((0, 0), (3, 3), (3, 3), (0, 0)))
    summed = jnp.zeros(features.shape, jnp.float32)
    for row_shift in range(7):
        for col_shift in range(7):
            summed = (
                summed
                + padded[:, row_shift : row_shift + height, col_shift : col_shift + breadth, :]
                * vectors[row_shift * 7 + col_shift]
            )
    return summed + vectors[49]


def normalize(features, vectors):
    conv = depthwise(features, vectors)
    average = jnp.mean(conv, axis=-1, keepdims=True)
    centered = conv - average
    variance = jnp.mean(centered * centered, axis=-1, keepdims=True)
    return centered * lax.rsqrt(variance + 1e-06) * vectors[50] + vectors[51]


def gelu_slope(preact):
    cumulative = 0.5 * (1.0 + jax.scipy.special.erf(preact * 0.7071067811865476))
    return cumulative + preact * jnp.exp(-0.5 * preact * preact) * 0.3989422804014327


def forward_block(features, first_weight, second_weight, vectors):
    width = features.shape[-1]
    normed = (
        normalize(features.astype(jnp.float32), vectors).astype(jnp.bfloat16).reshape(-1, width)
    )
    preact = jnp.dot(normed, first_weight, preferred_element_type=jnp.float32) + vectors[
        54:58
    ].reshape(-1)
    activated = jax.nn.gelu(preact, approximate=False).astype(jnp.bfloat16)
    projected = jnp.dot(activated, second_weight, preferred_element_type=jnp.float32) + vectors[52]
    output = (
        features.astype(jnp.float32) + vectors[53] * projected.reshape(features.shape)
    ).astype(jnp.bfloat16)
    return (output, normed, preact, activated, projected)


def backward_block(
    features, upstream, first_weight, second_weight, vectors, normed, preact, activated, projected
):
    width = features.shape[-1]
    flat_up = upstream.astype(jnp.float32).reshape(-1, width)
    grad_scale = jnp.sum(flat_up * projected, axis=0)
    dproj = flat_up * vectors[53]
    grad_bias_out = jnp.sum(dproj, axis=0)
    dproj_b = dproj.astype(jnp.bfloat16)
    grad_second = lax.dot_general(
        activated, dproj_b, (((0,), (0,)), ((), ())), preferred_element_type=jnp.float32
    )
    dact = lax.dot_general(
        dproj_b, second_weight, (((1,), (1,)), ((), ())), preferred_element_type=jnp.float32
    )
    dpre = dact * gelu_slope(preact)
    grad_bias_in = jnp.sum(dpre, axis=0)
    dpre_b = dpre.astype(jnp.bfloat16)
    grad_first = lax.dot_general(
        normed, dpre_b, (((0,), (0,)), ((), ())), preferred_element_type=jnp.float32
    )
    dnormed = lax.dot_general(
        dpre_b, first_weight, (((1,), (1,)), ((), ())), preferred_element_type=jnp.float32
    )
    unused, pullback = jax.vjp(normalize, features.astype(jnp.float32), vectors)
    grad_field, grad_small = pullback(dnormed.reshape(features.shape))
    grad_small = jnp.concatenate(
        [
            grad_small[:52],
            grad_small[52:53] + grad_bias_out[None],
            grad_small[53:54] + grad_scale[None],
            grad_small[54:58] + grad_bias_in.reshape(4, width),
        ]
    )
    down_grad = (grad_field + flat_up.reshape(features.shape)).astype(jnp.bfloat16)
    return (down_grad, grad_first, grad_second, grad_small)


def per_device(inputs, out_grad, w_in, w_out, vector_params):
    first_weight = w_in[0]
    second_weight = w_out[0]
    vectors = vector_params[0]
    section = lax.axis_index("segment")
    sections = lax.axis_size("segment")
    micro_count = inputs.shape[0]
    feature_shape = (micro_count * inputs.shape[1],) + inputs.shape[2:]
    batch_shape = inputs.shape
    width = feature_shape[-1]
    pixels = feature_shape[0] * feature_shape[1] * feature_shape[2]
    hidden = first_weight.shape[1]
    entering = inputs.reshape(feature_shape)
    leaving = out_grad.reshape(feature_shape)

    def run_forward(operands):
        features, stash = operands
        output, normed, preact, activated, projected = forward_block(
            features, first_weight, second_weight, vectors
        )
        return output, (features, normed, preact, activated, projected)

    def skip_forward(operands):
        features, stash = operands
        return jnp.zeros(feature_shape, jnp.bfloat16), stash

    stash = (
        jnp.zeros(feature_shape, jnp.bfloat16),
        jnp.zeros((pixels, width), jnp.bfloat16),
        jnp.zeros((pixels, hidden), jnp.float32),
        jnp.zeros((pixels, hidden), jnp.bfloat16),
        jnp.zeros((pixels, width), jnp.float32),
    )
    held = entering
    for tick_index in range(sections - 1):
        output, stash = lax.cond(section == tick_index, run_forward, skip_forward, (held, stash))
        held = from_behind(output, "segment", 1)

    def run_head(operands):
        upstream, kept, stash = operands
        features, normed, preact, activated, projected = stash
        flat_up = upstream.astype(jnp.float32).reshape(-1, width)
        grad_scale = jnp.sum(flat_up * projected, axis=0)
        dproj = flat_up * vectors[53]
        grad_bias_out = jnp.sum(dproj, axis=0)
        dproj_b = dproj.astype(jnp.bfloat16)
        dact = lax.dot_general(
            dproj_b, second_weight, (((1,), (1,)), ((), ())), preferred_element_type=jnp.float32
        )
        dpre = dact * gelu_slope(preact)
        grad_bias_in = jnp.sum(dpre, axis=0)
        dpre_b = dpre.astype(jnp.bfloat16)
        dnormed = lax.dot_general(
            dpre_b, first_weight, (((1,), (1,)), ((), ())), preferred_element_type=jnp.float32
        )
        return (dproj_b, dpre_b, dnormed, grad_scale, grad_bias_out, grad_bias_in)

    def skip_head(operands):
        upstream, kept = operands
        return kept

    def run_tail(operands):
        upstream, dnormed, kept, stash = operands
        features = stash[0]
        flat_up = upstream.astype(jnp.float32).reshape(-1, width)
        unused, pullback = jax.vjp(normalize, features.astype(jnp.float32), vectors)
        grad_field, grad_small = pullback(dnormed.reshape(features.shape))
        down_grad = (grad_field + flat_up.reshape(features.shape)).astype(jnp.bfloat16)
        return down_grad, grad_small

    def skip_tail(operands):
        upstream, dnormed, kept = operands
        return kept

    def run_both(operands):
        upstream, head, tail, stash = operands
        head = run_head((upstream, head, stash))
        return head, run_tail((upstream, head[2], tail, stash))

    def skip_both(operands):
        upstream, head, tail, stash = operands
        return head, tail

    def run_last(operands):
        features, upstream, head, tail, stash = operands
        unused, stash = run_forward((features, stash))
        head, tail = run_both((upstream, head, tail, stash))
        return head, tail, stash

    def skip_last(operands):
        features, upstream, head, tail, stash = operands
        return head, tail, stash

    head = (
        jnp.zeros((pixels, width), jnp.bfloat16),
        jnp.zeros((pixels, hidden), jnp.bfloat16),
        jnp.zeros((pixels, width), jnp.float32),
        jnp.zeros((width,), jnp.float32),
        jnp.zeros((width,), jnp.float32),
        jnp.zeros((hidden,), jnp.float32),
    )
    tail = (jnp.zeros(feature_shape, jnp.bfloat16), jnp.zeros(vectors.shape, jnp.float32))
    head, tail, stash = lax.cond(
        section == sections - 1, run_last, skip_last, (held, leaving, head, tail, stash)
    )
    held = from_behind(tail[0], "segment", -1)
    for tick_index in range(1, sections):
        active = section == sections - 1 - tick_index
        head, tail = lax.cond(active, run_both, skip_both, (held, head, tail, stash))
        if tick_index + 1 < sections:
            held = from_behind(tail[0], "segment", -1)
    kept = tail[0]
    dproj_b, dpre_b, unused, grad_scale, grad_bias_out, grad_bias_in = head
    features, normed, preact, activated, projected = stash
    acc_second = lax.dot_general(
        activated, dproj_b, (((0,), (0,)), ((), ())), preferred_element_type=jnp.float32
    )
    acc_first = lax.dot_general(
        normed, dpre_b, (((0,), (0,)), ((), ())), preferred_element_type=jnp.float32
    )
    grad_small = tail[1]
    acc_small = jnp.concatenate(
        [
            grad_small[:52],
            grad_small[52:53] + grad_bias_out[None],
            grad_small[53:54] + grad_scale[None],
            grad_small[54:58] + grad_bias_in.reshape(4, width),
        ]
    )
    params_total = sections * (first_weight.size + second_weight.size + vectors.size)
    sum_first, sum_second, sum_small = sum_over((acc_first, acc_second, acc_small), "dp")
    own_sum = (
        jnp.sum(sum_first * sum_first)
        + jnp.sum(sum_second * sum_second)
        + jnp.sum(sum_small * sum_small)
    )
    squares = lax.psum(own_sum, "segment")
    factor = jnp.minimum(1.0, jnp.sqrt(jnp.float32(params_total)) * lax.rsqrt(squares + 1e-06))
    step_first = factor * sum_first
    step_second = factor * sum_second
    step_small = factor * sum_small
    input_grads = kept.reshape(batch_shape)
    return (input_grads[None], step_first[None], step_second[None], step_small[None])


def solution(mesh):
    in_specs = (
        P(None, "dp", None, None, None),
        P(None, "dp", None, None, None),
        P("segment", None, None),
        P("segment", None, None),
        P("segment", None, None),
    )
    out_specs = (
        P("segment", None, "dp", None, None, None),
        P("segment", None, None),
        P("segment", None, None),
        P("segment", None, None),
    )
    return jax.shard_map(
        per_device, mesh=mesh, in_specs=in_specs, out_specs=out_specs, check_vma=False
    )
```

```python
import jax
import jax.numpy as jnp
from jax import lax
from jax.sharding import PartitionSpec as P


def from_behind(value, axis, by):
    devices = lax.axis_size(axis)
    pairs = [(i, i + by) for i in range(devices) if 0 <= i + by < devices]
    return lax.ppermute(value, axis, pairs)


def halving_reduce(parts, axis, orders):
    count = lax.axis_size(axis)
    me = lax.axis_index(axis)
    current = list(parts)
    for step in range(len(orders[0])):
        sides = []
        sends = []
        for index, piece in enumerate(current):
            bit = orders[index][step]
            side = (me >> bit) & 1
            halves = piece.reshape((2, piece.shape[0] // 2) + piece.shape[1:])
            sends.append(lax.dynamic_index_in_dim(halves, 1 - side, 0, keepdims=False))
            sides.append((side, halves))
        got = [
            lax.ppermute(send, axis, [(j, j ^ (1 << orders[index][step])) for j in range(count)])
            for index, send in enumerate(sends)
        ]
        current = [
            lax.dynamic_index_in_dim(halves, side, 0, keepdims=False) + received
            for (side, halves), received in zip(sides, got)
        ]
    return current


def doubling_gather(parts, axis, orders):
    count = lax.axis_size(axis)
    me = lax.axis_index(axis)
    current = list(parts)
    for step in reversed(range(len(orders[0]))):
        got = [
            lax.ppermute(piece, axis, [(j, j ^ (1 << orders[index][step])) for j in range(count)])
            for index, piece in enumerate(current)
        ]
        joined = []
        for index, (piece, received) in enumerate(zip(current, got)):
            side = (me >> orders[index][step]) & 1
            both = jnp.zeros((2,) + piece.shape, piece.dtype)
            both = lax.dynamic_update_index_in_dim(both, piece, side, 0)
            both = lax.dynamic_update_index_in_dim(both, received, 1 - side, 0)
            joined.append(both.reshape((2 * piece.shape[0],) + piece.shape[1:]))
        current = joined
    return current


def sum_over(arrays, axis):
    count = lax.axis_size(axis)
    bits = count.bit_length() - 1
    if count != 1 << bits or bits < 2:
        return lax.psum(tuple(arrays), axis)
    first_grad, second_grad, small_grad = arrays
    rows = second_grad.shape[0] + small_grad.shape[0]
    unit = 8 * count
    total = -(-rows // unit) * unit
    joined = jnp.concatenate(
        [second_grad, small_grad, jnp.zeros((total - rows, small_grad.shape[1]), small_grad.dtype)]
    )
    orders = (list(range(bits)), [1, 0] + list(range(2, bits)))
    shards = halving_reduce([first_grad, joined], axis, orders)
    first_sum, joined_sum = doubling_gather(shards, axis, orders)
    second_rows = second_grad.shape[0]
    return (
        first_sum,
        joined_sum[:second_rows],
        joined_sum[second_rows : second_rows + small_grad.shape[0]],
    )


def pairwise_total(value, axis):
    count = lax.axis_size(axis)
    bits = count.bit_length() - 1
    if count != 1 << bits:
        return lax.psum(value, axis)
    tile = jnp.broadcast_to(value, (8, 128)).astype(jnp.float32)
    for bit in range(bits):
        tile = tile + lax.ppermute(tile, axis, [(j, j ^ (1 << bit)) for j in range(count)])
    return tile[0, 0]


def depthwise(features, vectors):
    height = features.shape[1]
    breadth = features.shape[2]
    padded = jnp.pad(features, ((0, 0), (3, 3), (3, 3), (0, 0)))
    summed = jnp.zeros(features.shape, jnp.float32)
    for row_shift in range(7):
        for col_shift in range(7):
            summed = (
                summed
                + padded[:, row_shift : row_shift + height, col_shift : col_shift + breadth, :]
                * vectors[row_shift * 7 + col_shift]
            )
    return summed + vectors[49]


def normalize(features, vectors):
    conv = depthwise(features, vectors)
    average = jnp.mean(conv, axis=-1, keepdims=True)
    centered = conv - average
    variance = jnp.mean(centered * centered, axis=-1, keepdims=True)
    return centered * lax.rsqrt(variance + 1e-06) * vectors[50] + vectors[51]


def gelu_slope(preact):
    cumulative = 0.5 * (1.0 + jax.scipy.special.erf(preact * 0.7071067811865476))
    return cumulative + preact * jnp.exp(-0.5 * preact * preact) * 0.3989422804014327


def forward_block(features, first_weight, second_weight, vectors):
    width = features.shape[-1]
    normed = (
        normalize(features.astype(jnp.float32), vectors).astype(jnp.bfloat16).reshape(-1, width)
    )
    preact = jnp.dot(normed, first_weight, preferred_element_type=jnp.float32) + vectors[
        54:58
    ].reshape(-1)
    activated = jax.nn.gelu(preact, approximate=False).astype(jnp.bfloat16)
    projected = jnp.dot(activated, second_weight, preferred_element_type=jnp.float32) + vectors[52]
    output = (
        features.astype(jnp.float32) + vectors[53] * projected.reshape(features.shape)
    ).astype(jnp.bfloat16)
    return (output, normed, preact, activated, projected)


def backward_block(
    features, upstream, first_weight, second_weight, vectors, normed, preact, activated, projected
):
    width = features.shape[-1]
    flat_up = upstream.astype(jnp.float32).reshape(-1, width)
    grad_scale = jnp.sum(flat_up * projected, axis=0)
    dproj = flat_up * vectors[53]
    grad_bias_out = jnp.sum(dproj, axis=0)
    dproj_b = dproj.astype(jnp.bfloat16)
    grad_second = lax.dot_general(
        activated, dproj_b, (((0,), (0,)), ((), ())), preferred_element_type=jnp.float32
    )
    dact = lax.dot_general(
        dproj_b, second_weight, (((1,), (1,)), ((), ())), preferred_element_type=jnp.float32
    )
    dpre = dact * gelu_slope(preact)
    grad_bias_in = jnp.sum(dpre, axis=0)
    dpre_b = dpre.astype(jnp.bfloat16)
    grad_first = lax.dot_general(
        normed, dpre_b, (((0,), (0,)), ((), ())), preferred_element_type=jnp.float32
    )
    dnormed = lax.dot_general(
        dpre_b, first_weight, (((1,), (1,)), ((), ())), preferred_element_type=jnp.float32
    )
    unused, pullback = jax.vjp(normalize, features.astype(jnp.float32), vectors)
    grad_field, grad_small = pullback(dnormed.reshape(features.shape))
    grad_small = jnp.concatenate(
        [
            grad_small[:52],
            grad_small[52:53] + grad_bias_out[None],
            grad_small[53:54] + grad_scale[None],
            grad_small[54:58] + grad_bias_in.reshape(4, width),
        ]
    )
    down_grad = (grad_field + flat_up.reshape(features.shape)).astype(jnp.bfloat16)
    return (down_grad, grad_first, grad_second, grad_small)


def per_device(inputs, out_grad, w_in, w_out, vector_params):
    first_weight = w_in[0]
    second_weight = w_out[0]
    vectors = vector_params[0]
    section = lax.axis_index("segment")
    sections = lax.axis_size("segment")
    micro_count = inputs.shape[0]
    feature_shape = (micro_count * inputs.shape[1],) + inputs.shape[2:]
    batch_shape = inputs.shape
    width = feature_shape[-1]
    pixels = feature_shape[0] * feature_shape[1] * feature_shape[2]
    hidden = first_weight.shape[1]
    entering = inputs.reshape(feature_shape)
    leaving = out_grad.reshape(feature_shape)

    def run_forward(operands):
        features, stash = operands
        output, normed, preact, activated, projected = forward_block(
            features, first_weight, second_weight, vectors
        )
        return output, (features, normed, preact, activated, projected)

    def skip_forward(operands):
        features, stash = operands
        return jnp.zeros(feature_shape, jnp.bfloat16), stash

    stash = (
        jnp.zeros(feature_shape, jnp.bfloat16),
        jnp.zeros((pixels, width), jnp.bfloat16),
        jnp.zeros((pixels, hidden), jnp.float32),
        jnp.zeros((pixels, hidden), jnp.bfloat16),
        jnp.zeros((pixels, width), jnp.float32),
    )
    held = entering
    for tick_index in range(sections - 1):
        output, stash = lax.cond(section == tick_index, run_forward, skip_forward, (held, stash))
        held = from_behind(output, "segment", 1)

    def run_head(operands):
        upstream, kept, stash = operands
        features, normed, preact, activated, projected = stash
        flat_up = upstream.astype(jnp.float32).reshape(-1, width)
        grad_scale = jnp.sum(flat_up * projected, axis=0)
        dproj = flat_up * vectors[53]
        grad_bias_out = jnp.sum(dproj, axis=0)
        dproj_b = dproj.astype(jnp.bfloat16)
        dact = lax.dot_general(
            dproj_b, second_weight, (((1,), (1,)), ((), ())), preferred_element_type=jnp.float32
        )
        dpre = dact * gelu_slope(preact)
        grad_bias_in = jnp.sum(dpre, axis=0)
        dpre_b = dpre.astype(jnp.bfloat16)
        dnormed = lax.dot_general(
            dpre_b, first_weight, (((1,), (1,)), ((), ())), preferred_element_type=jnp.float32
        )
        return (dproj_b, dpre_b, dnormed, grad_scale, grad_bias_out, grad_bias_in)

    def skip_head(operands):
        upstream, kept = operands
        return kept

    def run_tail(operands):
        upstream, dnormed, kept, stash = operands
        features = stash[0]
        flat_up = upstream.astype(jnp.float32).reshape(-1, width)
        unused, pullback = jax.vjp(normalize, features.astype(jnp.float32), vectors)
        grad_field, grad_small = pullback(dnormed.reshape(features.shape))
        down_grad = (grad_field + flat_up.reshape(features.shape)).astype(jnp.bfloat16)
        return down_grad, grad_small

    def skip_tail(operands):
        upstream, dnormed, kept = operands
        return kept

    def run_both(operands):
        upstream, head, tail, stash = operands
        head = run_head((upstream, head, stash))
        return head, run_tail((upstream, head[2], tail, stash))

    def skip_both(operands):
        upstream, head, tail, stash = operands
        return head, tail

    def run_last(operands):
        features, upstream, head, tail, stash = operands
        unused, stash = run_forward((features, stash))
        head, tail = run_both((upstream, head, tail, stash))
        return head, tail, stash

    def skip_last(operands):
        features, upstream, head, tail, stash = operands
        return head, tail, stash

    head = (
        jnp.zeros((pixels, width), jnp.bfloat16),
        jnp.zeros((pixels, hidden), jnp.bfloat16),
        jnp.zeros((pixels, width), jnp.float32),
        jnp.zeros((width,), jnp.float32),
        jnp.zeros((width,), jnp.float32),
        jnp.zeros((hidden,), jnp.float32),
    )
    tail = (jnp.zeros(feature_shape, jnp.bfloat16), jnp.zeros(vectors.shape, jnp.float32))
    head, tail, stash = lax.cond(
        section == sections - 1, run_last, skip_last, (held, leaving, head, tail, stash)
    )
    held = from_behind(tail[0], "segment", -1)
    for tick_index in range(1, sections):
        active = section == sections - 1 - tick_index
        head, tail = lax.cond(active, run_both, skip_both, (held, head, tail, stash))
        if tick_index + 1 < sections:
            held = from_behind(tail[0], "segment", -1)
    kept = tail[0]
    dproj_b, dpre_b, unused, grad_scale, grad_bias_out, grad_bias_in = head
    features, normed, preact, activated, projected = stash
    acc_second = lax.dot_general(
        activated, dproj_b, (((0,), (0,)), ((), ())), preferred_element_type=jnp.float32
    )
    acc_first = lax.dot_general(
        normed, dpre_b, (((0,), (0,)), ((), ())), preferred_element_type=jnp.float32
    )
    grad_small = tail[1]
    acc_small = jnp.concatenate(
        [
            grad_small[:52],
            grad_small[52:53] + grad_bias_out[None],
            grad_small[53:54] + grad_scale[None],
            grad_small[54:58] + grad_bias_in.reshape(4, width),
        ]
    )
    params_total = sections * (first_weight.size + second_weight.size + vectors.size)
    sum_first, sum_second, sum_small = sum_over((acc_first, acc_second, acc_small), "dp")
    own_sum = (
        jnp.sum(sum_first * sum_first)
        + jnp.sum(sum_second * sum_second)
        + jnp.sum(sum_small * sum_small)
    )
    squares = pairwise_total(own_sum, "segment")
    factor = jnp.minimum(1.0, jnp.sqrt(jnp.float32(params_total)) * lax.rsqrt(squares + 1e-06))
    step_first = factor * sum_first
    step_second = factor * sum_second
    step_small = factor * sum_small
    input_grads = kept.reshape(batch_shape)
    return (input_grads[None], step_first[None], step_second[None], step_small[None])


def solution(mesh):
    in_specs = (
        P(None, "dp", None, None, None),
        P(None, "dp", None, None, None),
        P("segment", None, None),
        P("segment", None, None),
        P("segment", None, None),
    )
    out_specs = (
        P("segment", None, "dp", None, None, None),
        P("segment", None, None),
        P("segment", None, None),
        P("segment", None, None),
    )
    return jax.shard_map(
        per_device, mesh=mesh, in_specs=in_specs, out_specs=out_specs, check_vma=False
    )
```

```python
import jax
import jax.numpy as jnp
from jax import lax
from jax.sharding import PartitionSpec as P


def from_behind(value, axis, by):
    devices = lax.axis_size(axis)
    pairs = [(i, i + by) for i in range(devices) if 0 <= i + by < devices]
    return lax.ppermute(value, axis, pairs)


def halving_reduce(parts, axis, orders):
    count = lax.axis_size(axis)
    me = lax.axis_index(axis)
    current = list(parts)
    for step in range(len(orders[0])):
        sides = []
        sends = []
        for index, piece in enumerate(current):
            bit = orders[index][step]
            side = (me >> bit) & 1
            halves = piece.reshape((2, piece.shape[0] // 2) + piece.shape[1:])
            sends.append(lax.dynamic_index_in_dim(halves, 1 - side, 0, keepdims=False))
            sides.append((side, halves))
        got = [
            lax.ppermute(send, axis, [(j, j ^ (1 << orders[index][step])) for j in range(count)])
            for index, send in enumerate(sends)
        ]
        current = [
            lax.dynamic_index_in_dim(halves, side, 0, keepdims=False) + received
            for (side, halves), received in zip(sides, got)
        ]
    return current


def doubling_gather(parts, axis, orders):
    count = lax.axis_size(axis)
    me = lax.axis_index(axis)
    current = list(parts)
    for step in reversed(range(len(orders[0]))):
        got = [
            lax.ppermute(piece, axis, [(j, j ^ (1 << orders[index][step])) for j in range(count)])
            for index, piece in enumerate(current)
        ]
        joined = []
        for index, (piece, received) in enumerate(zip(current, got)):
            side = (me >> orders[index][step]) & 1
            both = jnp.zeros((2,) + piece.shape, piece.dtype)
            both = lax.dynamic_update_index_in_dim(both, piece, side, 0)
            both = lax.dynamic_update_index_in_dim(both, received, 1 - side, 0)
            joined.append(both.reshape((2 * piece.shape[0],) + piece.shape[1:]))
        current = joined
    return current


def sum_over(arrays, axis):
    count = lax.axis_size(axis)
    bits = count.bit_length() - 1
    if count != 1 << bits or bits < 2:
        return lax.psum(tuple(arrays), axis)
    first_grad, second_grad, small_grad = arrays
    rows = second_grad.shape[0] + small_grad.shape[0]
    unit = 8 * count
    total = -(-rows // unit) * unit
    joined = jnp.concatenate(
        [second_grad, small_grad, jnp.zeros((total - rows, small_grad.shape[1]), small_grad.dtype)]
    )
    orders = (list(range(bits)), list(range(1, bits)) + [0])
    shards = halving_reduce([first_grad, joined], axis, orders)
    first_sum, joined_sum = doubling_gather(shards, axis, orders)
    second_rows = second_grad.shape[0]
    return (
        first_sum,
        joined_sum[:second_rows],
        joined_sum[second_rows : second_rows + small_grad.shape[0]],
    )


def pairwise_total(value, axis):
    count = lax.axis_size(axis)
    bits = count.bit_length() - 1
    if count != 1 << bits:
        return lax.psum(value, axis)
    tile = jnp.broadcast_to(value, (8, 128)).astype(jnp.float32)
    for bit in range(bits):
        tile = tile + lax.ppermute(tile, axis, [(j, j ^ (1 << bit)) for j in range(count)])
    return tile[0, 0]


def depthwise(features, vectors):
    height = features.shape[1]
    breadth = features.shape[2]
    padded = jnp.pad(features, ((0, 0), (3, 3), (3, 3), (0, 0)))
    summed = jnp.zeros(features.shape, jnp.float32)
    for row_shift in range(7):
        for col_shift in range(7):
            summed = (
                summed
                + padded[:, row_shift : row_shift + height, col_shift : col_shift + breadth, :]
                * vectors[row_shift * 7 + col_shift]
            )
    return summed + vectors[49]


def normalize(features, vectors):
    conv = depthwise(features, vectors)
    average = jnp.mean(conv, axis=-1, keepdims=True)
    centered = conv - average
    variance = jnp.mean(centered * centered, axis=-1, keepdims=True)
    return centered * lax.rsqrt(variance + 1e-06) * vectors[50] + vectors[51]


def gelu_slope(preact):
    cumulative = 0.5 * (1.0 + jax.scipy.special.erf(preact * 0.7071067811865476))
    return cumulative + preact * jnp.exp(-0.5 * preact * preact) * 0.3989422804014327


def forward_block(features, first_weight, second_weight, vectors):
    width = features.shape[-1]
    normed = (
        normalize(features.astype(jnp.float32), vectors).astype(jnp.bfloat16).reshape(-1, width)
    )
    preact = jnp.dot(normed, first_weight, preferred_element_type=jnp.float32) + vectors[
        54:58
    ].reshape(-1)
    activated = jax.nn.gelu(preact, approximate=False).astype(jnp.bfloat16)
    projected = jnp.dot(activated, second_weight, preferred_element_type=jnp.float32) + vectors[52]
    output = (
        features.astype(jnp.float32) + vectors[53] * projected.reshape(features.shape)
    ).astype(jnp.bfloat16)
    return (output, normed, preact, activated, projected)


def backward_block(
    features, upstream, first_weight, second_weight, vectors, normed, preact, activated, projected
):
    width = features.shape[-1]
    flat_up = upstream.astype(jnp.float32).reshape(-1, width)
    grad_scale = jnp.sum(flat_up * projected, axis=0)
    dproj = flat_up * vectors[53]
    grad_bias_out = jnp.sum(dproj, axis=0)
    dproj_b = dproj.astype(jnp.bfloat16)
    grad_second = lax.dot_general(
        activated, dproj_b, (((0,), (0,)), ((), ())), preferred_element_type=jnp.float32
    )
    dact = lax.dot_general(
        dproj_b, second_weight, (((1,), (1,)), ((), ())), preferred_element_type=jnp.float32
    )
    dpre = dact * gelu_slope(preact)
    grad_bias_in = jnp.sum(dpre, axis=0)
    dpre_b = dpre.astype(jnp.bfloat16)
    grad_first = lax.dot_general(
        normed, dpre_b, (((0,), (0,)), ((), ())), preferred_element_type=jnp.float32
    )
    dnormed = lax.dot_general(
        dpre_b, first_weight, (((1,), (1,)), ((), ())), preferred_element_type=jnp.float32
    )
    unused, pullback = jax.vjp(normalize, features.astype(jnp.float32), vectors)
    grad_field, grad_small = pullback(dnormed.reshape(features.shape))
    grad_small = jnp.concatenate(
        [
            grad_small[:52],
            grad_small[52:53] + grad_bias_out[None],
            grad_small[53:54] + grad_scale[None],
            grad_small[54:58] + grad_bias_in.reshape(4, width),
        ]
    )
    down_grad = (grad_field + flat_up.reshape(features.shape)).astype(jnp.bfloat16)
    return (down_grad, grad_first, grad_second, grad_small)


def per_device(inputs, out_grad, w_in, w_out, vector_params):
    first_weight = w_in[0]
    second_weight = w_out[0]
    vectors = vector_params[0]
    section = lax.axis_index("segment")
    sections = lax.axis_size("segment")
    micro_count = inputs.shape[0]
    feature_shape = (micro_count * inputs.shape[1],) + inputs.shape[2:]
    batch_shape = inputs.shape
    width = feature_shape[-1]
    pixels = feature_shape[0] * feature_shape[1] * feature_shape[2]
    hidden = first_weight.shape[1]
    entering = inputs.reshape(feature_shape)
    leaving = out_grad.reshape(feature_shape)

    def run_forward(operands):
        features, stash = operands
        output, normed, preact, activated, projected = forward_block(
            features, first_weight, second_weight, vectors
        )
        return output, (features, normed, preact, activated, projected)

    def skip_forward(operands):
        features, stash = operands
        return jnp.zeros(feature_shape, jnp.bfloat16), stash

    stash = (
        jnp.zeros(feature_shape, jnp.bfloat16),
        jnp.zeros((pixels, width), jnp.bfloat16),
        jnp.zeros((pixels, hidden), jnp.float32),
        jnp.zeros((pixels, hidden), jnp.bfloat16),
        jnp.zeros((pixels, width), jnp.float32),
    )
    held = entering
    for tick_index in range(sections - 1):
        output, stash = lax.cond(section == tick_index, run_forward, skip_forward, (held, stash))
        held = from_behind(output, "segment", 1)

    def run_head(operands):
        upstream, kept, stash = operands
        features, normed, preact, activated, projected = stash
        flat_up = upstream.astype(jnp.float32).reshape(-1, width)
        grad_scale = jnp.sum(flat_up * projected, axis=0)
        dproj = flat_up * vectors[53]
        grad_bias_out = jnp.sum(dproj, axis=0)
        dproj_b = dproj.astype(jnp.bfloat16)
        dact = lax.dot_general(
            dproj_b, second_weight, (((1,), (1,)), ((), ())), preferred_element_type=jnp.float32
        )
        dpre = dact * gelu_slope(preact)
        grad_bias_in = jnp.sum(dpre, axis=0)
        dpre_b = dpre.astype(jnp.bfloat16)
        dnormed = lax.dot_general(
            dpre_b, first_weight, (((1,), (1,)), ((), ())), preferred_element_type=jnp.float32
        )
        return (dproj_b, dpre_b, dnormed, grad_scale, grad_bias_out, grad_bias_in)

    def skip_head(operands):
        upstream, kept = operands
        return kept

    def run_tail(operands):
        upstream, dnormed, kept, stash = operands
        features = stash[0]
        flat_up = upstream.astype(jnp.float32).reshape(-1, width)
        unused, pullback = jax.vjp(normalize, features.astype(jnp.float32), vectors)
        grad_field, grad_small = pullback(dnormed.reshape(features.shape))
        down_grad = (grad_field + flat_up.reshape(features.shape)).astype(jnp.bfloat16)
        return down_grad, grad_small

    def skip_tail(operands):
        upstream, dnormed, kept = operands
        return kept

    def run_both(operands):
        upstream, head, tail, stash = operands
        head = run_head((upstream, head, stash))
        return head, run_tail((upstream, head[2], tail, stash))

    def skip_both(operands):
        upstream, head, tail, stash = operands
        return head, tail

    def run_last(operands):
        features, upstream, head, tail, stash = operands
        unused, stash = run_forward((features, stash))
        head, tail = run_both((upstream, head, tail, stash))
        return head, tail, stash

    def skip_last(operands):
        features, upstream, head, tail, stash = operands
        return head, tail, stash

    head = (
        jnp.zeros((pixels, width), jnp.bfloat16),
        jnp.zeros((pixels, hidden), jnp.bfloat16),
        jnp.zeros((pixels, width), jnp.float32),
        jnp.zeros((width,), jnp.float32),
        jnp.zeros((width,), jnp.float32),
        jnp.zeros((hidden,), jnp.float32),
    )
    tail = (jnp.zeros(feature_shape, jnp.bfloat16), jnp.zeros(vectors.shape, jnp.float32))
    head, tail, stash = lax.cond(
        section == sections - 1, run_last, skip_last, (held, leaving, head, tail, stash)
    )
    held = from_behind(tail[0], "segment", -1)
    for tick_index in range(1, sections):
        active = section == sections - 1 - tick_index
        head, tail = lax.cond(active, run_both, skip_both, (held, head, tail, stash))
        if tick_index + 1 < sections:
            held = from_behind(tail[0], "segment", -1)
    kept = tail[0]
    dproj_b, dpre_b, unused, grad_scale, grad_bias_out, grad_bias_in = head
    features, normed, preact, activated, projected = stash
    acc_second = lax.dot_general(
        activated, dproj_b, (((0,), (0,)), ((), ())), preferred_element_type=jnp.float32
    )
    acc_first = lax.dot_general(
        normed, dpre_b, (((0,), (0,)), ((), ())), preferred_element_type=jnp.float32
    )
    grad_small = tail[1]
    acc_small = jnp.concatenate(
        [
            grad_small[:52],
            grad_small[52:53] + grad_bias_out[None],
            grad_small[53:54] + grad_scale[None],
            grad_small[54:58] + grad_bias_in.reshape(4, width),
        ]
    )
    params_total = sections * (first_weight.size + second_weight.size + vectors.size)
    sum_first, sum_second, sum_small = sum_over((acc_first, acc_second, acc_small), "dp")
    own_sum = (
        jnp.sum(sum_first * sum_first)
        + jnp.sum(sum_second * sum_second)
        + jnp.sum(sum_small * sum_small)
    )
    squares = pairwise_total(own_sum, "segment")
    factor = jnp.minimum(1.0, jnp.sqrt(jnp.float32(params_total)) * lax.rsqrt(squares + 1e-06))
    step_first = factor * sum_first
    step_second = factor * sum_second
    step_small = factor * sum_small
    input_grads = kept.reshape(batch_shape)
    return (input_grads[None], step_first[None], step_second[None], step_small[None])


def solution(mesh):
    in_specs = (
        P(None, "dp", None, None, None),
        P(None, "dp", None, None, None),
        P("segment", None, None),
        P("segment", None, None),
        P("segment", None, None),
    )
    out_specs = (
        P("segment", None, "dp", None, None, None),
        P("segment", None, None),
        P("segment", None, None),
        P("segment", None, None),
    )
    return jax.shard_map(
        per_device, mesh=mesh, in_specs=in_specs, out_specs=out_specs, check_vma=False
    )
```
